32 devices in a mesh: uv: 8 (over z, y), tm: 4 (over x, core).
Axes of the slice: x: 2, y: 2, z: 4, core: 2. Of those that a mesh axis runs over, the one named last changes fastest.
Arguments:
- visibility: bfloat16 [4, 1024, 2048], P('tm', 'uv'), may hold values from -1536 to 1536
- anchor: int32 [4, 1024], P('tm', 'uv'), may hold values from 0 to 80
- offset: int32 [4, 1024], P('tm', 'uv'), may hold values from 0 to 63
- slot_rows: int32 [4, 8, 8, 32], P('tm', 'uv'), may hold values from 0 to 127, as said below
- counts: int32 [4, 8, 8], P('tm', 'uv'), may hold values from 0 to 32, as said below
Outputs:
- delay: float32 [2048, 2048], P(('uv', 'tm'))
The draws below stay inside these ranges and needn't reach their ends.
Inputs may be any that keep to these rules, and one draw needn't show every extreme that they name: For every g and s the first counts[g, s, d] entries of slot_rows[g, s, d] over all d name each of the 128 rows of device s exactly once; entries at slots k >= counts[g, s, d] are arbitrary rows and are not used. counts[g, s, :] sums to 128; in each time group one tile receives 32 rows from every device and another tile none; the other tiles come in pairs whose counts from one device sum to 32.
All inputs are finite; a program needn't handle non-finite values.
Results may differ from the reference program's by a relative error of at most 0.0047.
Values may be sent and summed in bfloat16 or wider, within the bound.
No kernel may reach another device: no remote copies, remote signals or barrier semaphores. Data moves between devices by JAX's collectives and lax.ppermute only.
A program may use at most 64 MiB of HBM per device.

```python
import math
import jax
import jax.numpy as jnp
from jax import lax

NCH = 1024
ROWS_DEV = 128
TS = 16
KTAPS = 8
OSAMP = 8
TILES = 8
GROUPS = 4
CAP = 32


def routing_plan(key):
    base_key = jax.random.fold_in(key, 7)
    key_order, key_delta, key_rows, key_spare = jax.random.split(base_key, 4)
    half_cap = ROWS_DEV // TILES
    tile_order = jax.vmap(lambda one_key: jax.random.permutation(one_key, TILES))(jax.random.split(key_order, GROUPS)).astype(jnp.int32)
    delta = jax.random.randint(key_delta, (GROUPS, TILES, (TILES - 2) // 2), 0, half_cap + 1).astype(jnp.int32)
    paired = jnp.stack([half_cap + delta, half_cap - delta], axis=-1).reshape(GROUPS, TILES, TILES - 2)
    leading = jnp.broadcast_to(jnp.array([2 * half_cap, 0], dtype=jnp.int32), (GROUPS, TILES, 2))
    in_order = jnp.concatenate([leading, paired], axis=-1).astype(jnp.int32)
    inverse = jnp.argsort(tile_order, axis=-1).astype(jnp.int32)
    count_table = jnp.take_along_axis(in_order, jnp.broadcast_to(inverse[:, None, :], (GROUPS, TILES, TILES)), axis=-1).astype(jnp.int32)
    row_order = jax.vmap(lambda one_key: jax.random.permutation(one_key, ROWS_DEV))(jax.random.split(key_rows, GROUPS * TILES)).reshape(GROUPS, TILES, ROWS_DEV).astype(jnp.int32)
    starts = jnp.cumsum(count_table, axis=-1) - count_table
    position = starts[..., None] + jnp.arange(CAP, dtype=jnp.int32)[None, None, None, :]
    position = jnp.minimum(position, ROWS_DEV - 1).reshape(GROUPS, TILES, TILES * CAP)
    filled = jnp.take_along_axis(row_order, position, axis=-1).reshape(GROUPS, TILES, TILES, CAP)
    spare = jax.random.randint(key_spare, (GROUPS, TILES, TILES, CAP), 0, ROWS_DEV).astype(jnp.int32)
    used = jnp.arange(CAP, dtype=jnp.int32)[None, None, None, :] < count_table[..., None]
    return (jnp.where(used, filled, spare).astype(jnp.int32), count_table)


def draw_slot_rows(key, part):
    return routing_plan(key)[0]


def draw_counts(key, part):
    return routing_plan(key)[1]


def draw_visibility(key, part):
    key_values, key_rough = jax.random.split(jax.random.fold_in(key, 11))
    shape = (GROUPS, TILES * ROWS_DEV, 2 * NCH)
    values = jnp.clip(jax.random.normal(key_values, shape, jnp.float32), -6.0, 6.0)
    freq = jnp.arange(NCH, dtype=jnp.float32)
    window_arg = 2.0 * math.pi * freq / (NCH - 1)
    taper = 0.35875 - 0.48829 * jnp.cos(window_arg) + 0.14128 * jnp.cos(2.0 * window_arg) - 0.01168 * jnp.cos(3.0 * window_arg)
    channel_gain = jnp.clip(0.1 / jnp.maximum(taper, 0.0001), 1.0, 128.0)
    rough = jnp.exp(jax.random.uniform(key_rough, (NCH,), jnp.float32, -0.69, 0.69))
    scaled = channel_gain * rough
    both_parts = jnp.concatenate([scaled, scaled], axis=0)
    return (values * both_parts[None, None, :]).astype(jnp.bfloat16)


def plant(entries, stream_key, smallest, high):
    spot = [jax.random.randint(jax.random.fold_in(stream_key, axis), (), 0, length) for axis, length in enumerate(entries.shape)]
    longest = entries.shape.index(max(entries.shape))
    beside = spot[:longest] + [(spot[longest] + 1) % entries.shape[longest]] + spot[longest + 1:]
    return entries.at[tuple(spot)].set(smallest).at[tuple(beside)].set(high)


def setup_inputs(seed: int = 0) -> dict:
    keys = jax.random.split(jax.random.key(seed), 6)
    return {
        "visibility": draw_visibility(jax.random.fold_in(keys[5], 71), 0),
        "anchor": plant(jax.random.randint(keys[1], (GROUPS, TILES * ROWS_DEV), 0, (TS - KTAPS + 1) * (TS - KTAPS + 1)), jax.random.fold_in(keys[1], 1), 0, ((TS - KTAPS + 1) * (TS - KTAPS + 1)) - 1).astype(jnp.int32),
        "offset": plant(jax.random.randint(keys[2], (GROUPS, TILES * ROWS_DEV), 0, OSAMP * OSAMP), jax.random.fold_in(keys[2], 1), 0, (OSAMP * OSAMP) - 1).astype(jnp.int32),
        "slot_rows": draw_slot_rows(jax.random.fold_in(keys[5], 71), 0),
        "counts": draw_counts(jax.random.fold_in(keys[5], 71), 0),
    }


def kernel_taps(offsets):
    tap_index = jnp.arange(KTAPS, dtype=jnp.float32)
    sub_shift = (offsets.astype(jnp.float32) + 0.5) / OSAMP
    distance = tap_index[None, :] - (KTAPS / 2 - 1.0) - sub_shift[:, None]
    return jnp.exp(-distance * distance / (2.0 * 1.2 * 1.2))

def tap_matrix(cell_ids, anchors, offsets):
    span = TS - KTAPS + 1
    anchor_y = anchors // span
    anchor_x = anchors % span
    taps_y = kernel_taps(offsets // OSAMP)
    taps_x = kernel_taps(offsets % OSAMP)
    cell_y = cell_ids // TS
    cell_x = cell_ids % TS
    along_y = jnp.zeros((cell_ids.shape[0], anchors.shape[0]), jnp.float32)
    along_x = jnp.zeros((cell_ids.shape[0], anchors.shape[0]), jnp.float32)
    for step in range(KTAPS):
        along_y = along_y + jnp.where(cell_y[:, None] == anchor_y[None, :] + step, taps_y[None, :, step], 0.0)
        along_x = along_x + jnp.where(cell_x[:, None] == anchor_x[None, :] + step, taps_x[None, :, step], 0.0)
    return (along_y * along_x).astype(jnp.bfloat16)

def delay_table():
    freq = jnp.arange(NCH, dtype=jnp.int32)
    phase = freq[:, None] * freq[None, :] % NCH
    angle = 2.0 * math.pi / NCH * phase.astype(jnp.float32)
    cosine = jnp.cos(angle)
    sine = jnp.sin(angle)
    window_arg = 2.0 * math.pi * freq.astype(jnp.float32) / (NCH - 1)
    taper = 0.35875 - 0.48829 * jnp.cos(window_arg) + 0.14128 * jnp.cos(2.0 * window_arg) - 0.01168 * jnp.cos(3.0 * window_arg)
    tap_cos = taper[:, None] * cosine
    tap_sin = taper[:, None] * sine
    upper = jnp.concatenate([tap_cos, -tap_sin], axis=1)
    lower = jnp.concatenate([tap_sin, tap_cos], axis=1)
    return jnp.concatenate([upper, lower], axis=0).astype(jnp.bfloat16)

def reference(visibility, anchor, offset, slot_rows, counts):
    cell_ids = jnp.arange(TS * TS, dtype=jnp.int32)
    transform = delay_table()
    out_scale = 4.0 / math.sqrt(NCH * GROUPS * ROWS_DEV)
    is_live = jnp.arange(CAP, dtype=jnp.int32)[None, None, None, :] < counts[..., None]
    row_base = (jnp.arange(TILES, dtype=jnp.int32) * ROWS_DEV)[None, :, None, None]
    global_rows = (slot_rows + row_base).astype(jnp.int32)

    def one_tile(tile):
        picked = global_rows[:, :, tile, :].reshape(GROUPS, -1)
        live_mask = is_live[:, :, tile, :].reshape(GROUPS, -1)
        tile_vis = jax.vmap(lambda vis_group, idx: jnp.take(vis_group, idx, axis=0))(visibility, picked)
        tile_vis = jnp.where(live_mask[..., None], tile_vis, jnp.zeros((), visibility.dtype))
        tile_anchor = jax.vmap(lambda group_a, idx: jnp.take(group_a, idx))(anchor, picked)
        tile_offset = jax.vmap(lambda group_o, idx: jnp.take(group_o, idx))(offset, picked)
        weights = tap_matrix(cell_ids, tile_anchor.reshape(-1), tile_offset.reshape(-1))
        grid = jnp.dot(weights, tile_vis.reshape(-1, 2 * NCH), preferred_element_type=jnp.float32).astype(jnp.bfloat16)
        return jnp.dot(grid, transform, preferred_element_type=jnp.float32) * out_scale
    stacked = lax.map(one_tile, jnp.arange(TILES, dtype=jnp.int32))
    return stacked.reshape(TILES * TS * TS, 2 * NCH)
```

```python
import math

import jax
import jax.numpy as jnp
from jax import lax
from jax.sharding import PartitionSpec as P

NCH = 1024
ROWS_DEV = 128
TS = 16
KTAPS = 8
OSAMP = 8
META = 128
SPLIT = 32


def kernel_taps(offsets):
    tap_index = jnp.arange(KTAPS, dtype=jnp.float32)
    sub_shift = (offsets.astype(jnp.float32) + 0.5) / OSAMP
    distance = tap_index[None, :] - (KTAPS / 2 - 1.0) - sub_shift[:, None]
    return jnp.exp(-distance * distance / (2.0 * 1.2 * 1.2))


def tap_matrix(cell_ids, anchors, offsets):
    span = TS - KTAPS + 1
    anchor_y = anchors // span
    anchor_x = anchors % span
    taps_y = kernel_taps(offsets // OSAMP)
    taps_x = kernel_taps(offsets % OSAMP)
    cell_y = cell_ids // TS
    cell_x = cell_ids % TS
    along_y = jnp.zeros((cell_ids.shape[0], anchors.shape[0]), jnp.float32)
    along_x = jnp.zeros((cell_ids.shape[0], anchors.shape[0]), jnp.float32)
    for step in range(KTAPS):
        along_y = along_y + jnp.where(
            cell_y[:, None] == anchor_y[None, :] + step, taps_y[None, :, step], 0.0
        )
        along_x = along_x + jnp.where(
            cell_x[:, None] == anchor_x[None, :] + step, taps_x[None, :, step], 0.0
        )
    return (along_y * along_x).astype(jnp.bfloat16)


def delay_halves():
    freq = jnp.arange(NCH, dtype=jnp.int32)
    hi = jnp.arange(NCH // SPLIT, dtype=jnp.int32)
    lo = jnp.arange(SPLIT, dtype=jnp.int32)
    scale = 2.0 * math.pi / NCH
    ang_hi = scale * ((freq[:, None] * (SPLIT * hi)[None, :]) % NCH).astype(jnp.float32)
    ang_lo = scale * ((freq[:, None] * lo[None, :]) % NCH).astype(jnp.float32)
    c_hi, s_hi = jnp.cos(ang_hi), jnp.sin(ang_hi)
    c_lo, s_lo = jnp.cos(ang_lo), jnp.sin(ang_lo)
    cosine = c_hi[:, :, None] * c_lo[:, None, :] - s_hi[:, :, None] * s_lo[:, None, :]
    sine = s_hi[:, :, None] * c_lo[:, None, :] + c_hi[:, :, None] * s_lo[:, None, :]
    window_arg = 2.0 * math.pi * freq.astype(jnp.float32) / (NCH - 1)
    taper = (
        0.35875
        - 0.48829 * jnp.cos(window_arg)
        + 0.14128 * jnp.cos(2.0 * window_arg)
        - 0.01168 * jnp.cos(3.0 * window_arg)
    )
    tap_cos = (taper[:, None, None] * cosine).reshape(NCH, NCH)
    tap_sin = (taper[:, None, None] * sine).reshape(NCH, NCH)
    return jnp.concatenate([tap_cos, tap_sin], axis=0).astype(jnp.bfloat16)


def per_device(visibility, anchor, offset, slot_rows, counts):
    time_groups = lax.axis_size("tm")
    vis_rows = visibility[0]
    row_width = vis_rows.shape[1]
    slot_table = slot_rows[0, 0]
    tile_count, slot_depth = slot_table.shape
    is_live = (jnp.arange(slot_depth, dtype=jnp.int32)[None, :] < counts[0, 0][:, None]).reshape(-1)
    flat_index = slot_table.reshape(-1)
    picked = jnp.where(
        is_live[:, None], jnp.take(vis_rows, flat_index, axis=0), jnp.zeros((), vis_rows.dtype)
    )
    out_anchor = jnp.take(anchor[0], flat_index).astype(jnp.bfloat16)
    out_offset = jnp.take(offset[0], flat_index).astype(jnp.bfloat16)
    meta = jnp.zeros((flat_index.shape[0], META), jnp.bfloat16)
    meta = meta.at[:, 0].set(out_anchor).at[:, 1].set(out_offset)
    outgoing = jnp.concatenate([picked, meta], axis=1).reshape(tile_count, slot_depth, row_width + META)
    arrived = lax.all_to_all(outgoing, "uv", split_axis=0, concat_axis=0, tiled=True)
    arrived = arrived.reshape(-1, row_width + META)
    arr_anchor = arrived[:, row_width].astype(jnp.int32)
    arr_offset = arrived[:, row_width + 1].astype(jnp.int32)
    all_cells = jnp.arange(TS * TS, dtype=jnp.int32)
    weights = tap_matrix(all_cells, arr_anchor, arr_offset)
    partial = jnp.dot(weights, arrived[:, :row_width], preferred_element_type=jnp.float32)
    summed = lax.psum_scatter(partial, "tm", scatter_dimension=0, tiled=True)
    grid = summed.astype(jnp.bfloat16)
    grid_re, grid_im = grid[:, :NCH], grid[:, NCH:]
    lhs = jnp.concatenate(
        [grid, jnp.concatenate([grid_im, -grid_re], axis=1)], axis=0
    )
    out_scale = 4.0 / math.sqrt(NCH * time_groups * ROWS_DEV)
    both = jnp.dot(lhs, delay_halves(), preferred_element_type=jnp.float32) * out_scale
    cells = grid.shape[0]
    return jnp.concatenate([both[:cells], both[cells:]], axis=1)


def solution(mesh):
    in_specs = (
        P("tm", "uv", None),
        P("tm", "uv"),
        P("tm", "uv"),
        P("tm", "uv", None, None),
        P("tm", "uv", None),
    )
    out_specs = P(("uv", "tm"), None)
    return jax.shard_map(
        per_device, mesh=mesh, in_specs=in_specs, out_specs=out_specs, check_vma=False
    )
```

```python
import math

import jax
import jax.numpy as jnp
from jax import lax
from jax.sharding import PartitionSpec as P

NCH = 1024
ROWS_DEV = 128
TS = 16
KTAPS = 8
OSAMP = 8
META = 128
SPLIT = 32


def kernel_taps(offsets):
    tap_index = jnp.arange(KTAPS, dtype=jnp.float32)
    sub_shift = (offsets.astype(jnp.float32) + 0.5) / OSAMP
    distance = tap_index[None, :] - (KTAPS / 2 - 1.0) - sub_shift[:, None]
    return jnp.exp(-distance * distance / (2.0 * 1.2 * 1.2))


def tap_matrix(cell_ids, anchors, offsets):
    span = TS - KTAPS + 1
    anchor_y = anchors // span
    anchor_x = anchors % span
    taps_y = kernel_taps(offsets // OSAMP)
    taps_x = kernel_taps(offsets % OSAMP)
    cell_y = cell_ids // TS
    cell_x = cell_ids % TS
    along_y = jnp.zeros((cell_ids.shape[0], anchors.shape[0]), jnp.float32)
    along_x = jnp.zeros((cell_ids.shape[0], anchors.shape[0]), jnp.float32)
    for step in range(KTAPS):
        along_y = along_y + jnp.where(
            cell_y[:, None] == anchor_y[None, :] + step, taps_y[None, :, step], 0.0
        )
        along_x = along_x + jnp.where(
            cell_x[:, None] == anchor_x[None, :] + step, taps_x[None, :, step], 0.0
        )
    return (along_y * along_x).astype(jnp.bfloat16)


def delay_halves():
    freq = jnp.arange(NCH, dtype=jnp.int32)
    hi = jnp.arange(NCH // SPLIT, dtype=jnp.int32)
    lo = jnp.arange(SPLIT, dtype=jnp.int32)
    scale = 2.0 * math.pi / NCH
    ang_hi = scale * ((freq[:, None] * (SPLIT * hi)[None, :]) % NCH).astype(jnp.float32)
    ang_lo = scale * ((freq[:, None] * lo[None, :]) % NCH).astype(jnp.float32)
    c_hi, s_hi = jnp.cos(ang_hi), jnp.sin(ang_hi)
    c_lo, s_lo = jnp.cos(ang_lo), jnp.sin(ang_lo)
    cosine = c_hi[:, :, None] * c_lo[:, None, :] - s_hi[:, :, None] * s_lo[:, None, :]
    sine = s_hi[:, :, None] * c_lo[:, None, :] + c_hi[:, :, None] * s_lo[:, None, :]
    window_arg = 2.0 * math.pi * freq.astype(jnp.float32) / (NCH - 1)
    taper = (
        0.35875
        - 0.48829 * jnp.cos(window_arg)
        + 0.14128 * jnp.cos(2.0 * window_arg)
        - 0.01168 * jnp.cos(3.0 * window_arg)
    )
    tap_cos = (taper[:, None, None] * cosine).reshape(NCH, NCH)
    tap_sin = (taper[:, None, None] * sine).reshape(NCH, NCH)
    return jnp.concatenate([tap_cos, tap_sin], axis=0).astype(jnp.bfloat16)


def halving_order(tm_index, time_groups, cell_share):
    level_bits = int(math.log2(time_groups))
    quarter = jnp.zeros((time_groups,), jnp.int32)
    for j in range(time_groups):
        value = tm_index
        pos = j
        for level in range(level_bits):
            half = time_groups >> (level + 1)
            sent = pos < half
            bit = 1 << level
            value = jnp.where(sent, value ^ bit, value)
            pos = pos % half if half > 0 else pos
        quarter = quarter.at[j].set(value)
    cells = quarter[:, None] * cell_share + jnp.arange(cell_share, dtype=jnp.int32)[None, :]
    return cells.reshape(-1)


def halving_reduce(partial, time_groups):
    level_bits = int(math.log2(time_groups))
    for level in range(level_bits):
        half = partial.shape[0] // 2
        bit = 1 << level
        perm = [(i, i ^ bit) for i in range(time_groups)]
        received = lax.ppermute(partial[:half], "tm", perm)
        partial = partial[half:] + received
    return partial


def per_device(visibility, anchor, offset, slot_rows, counts):
    time_groups = lax.axis_size("tm")
    cell_share = TS * TS // time_groups
    vis_rows = visibility[0]
    row_count, row_width = vis_rows.shape
    slot_table = slot_rows[0, 0]
    tile_count, slot_depth = slot_table.shape
    is_live = (jnp.arange(slot_depth, dtype=jnp.int32)[None, :] < counts[0, 0][:, None]).reshape(-1)
    flat_index = slot_table.reshape(-1)
    pick = (
        (flat_index[:, None] == jnp.arange(row_count, dtype=jnp.int32)[None, :]) & is_live[:, None]
    ).astype(jnp.bfloat16)
    picked = jnp.dot(pick, vis_rows, preferred_element_type=jnp.float32).astype(jnp.bfloat16)
    meta_src = jnp.zeros((row_count, META), jnp.float32)
    meta_src = meta_src.at[:, 0].set(anchor[0].astype(jnp.float32))
    meta_src = meta_src.at[:, 1].set(offset[0].astype(jnp.float32))
    meta = jnp.dot(pick, meta_src.astype(jnp.bfloat16), preferred_element_type=jnp.float32)
    meta = meta.astype(jnp.bfloat16)
    outgoing = jnp.concatenate([picked, meta], axis=1).reshape(tile_count, slot_depth, row_width + META)
    arrived = lax.all_to_all(outgoing, "uv", split_axis=0, concat_axis=0, tiled=True)
    arrived = arrived.reshape(-1, row_width + META)
    arr_anchor = arrived[:, row_width].astype(jnp.int32)
    arr_offset = arrived[:, row_width + 1].astype(jnp.int32)
    tm_index = lax.axis_index("tm")
    if time_groups & (time_groups - 1) == 0:
        cells = halving_order(tm_index, time_groups, cell_share)
    else:
        cells = jnp.arange(TS * TS, dtype=jnp.int32)
    weights = tap_matrix(cells, arr_anchor, arr_offset)
    partial = jnp.dot(weights, arrived[:, :row_width], preferred_element_type=jnp.float32)
    if time_groups & (time_groups - 1) == 0:
        summed = halving_reduce(partial, time_groups)
    else:
        summed = lax.psum_scatter(partial, "tm", scatter_dimension=0, tiled=True)
    grid = summed.astype(jnp.bfloat16)
    grid_re, grid_im = grid[:, :NCH], grid[:, NCH:]
    lhs = jnp.concatenate(
        [grid, jnp.concatenate([grid_im, -grid_re], axis=1)], axis=0
    )
    out_scale = 4.0 / math.sqrt(NCH * time_groups * ROWS_DEV)
    both = jnp.dot(lhs, delay_halves(), preferred_element_type=jnp.float32) * out_scale
    cells_out = grid.shape[0]
    return jnp.concatenate([both[:cells_out], both[cells_out:]], axis=1)


def solution(mesh):
    in_specs = (
        P("tm", "uv", None),
        P("tm", "uv"),
        P("tm", "uv"),
        P("tm", "uv", None, None),
        P("tm", "uv", None),
    )
    out_specs = P(("uv", "tm"), None)
    return jax.shard_map(
        per_device, mesh=mesh, in_specs=in_specs, out_specs=out_specs, check_vma=False
    )
```

```python
import math

import jax
import jax.numpy as jnp
from jax import lax
from jax.sharding import PartitionSpec as P

NCH = 1024
ROWS_DEV = 128
TS = 16
KTAPS = 8
OSAMP = 8
META = 128
SPLIT = 32
CHUNKS = 2


def kernel_taps(offsets):
    tap_index = jnp.arange(KTAPS, dtype=jnp.float32)
    sub_shift = (offsets.astype(jnp.float32) + 0.5) / OSAMP
    distance = tap_index[None, :] - (KTAPS / 2 - 1.0) - sub_shift[:, None]
    return jnp.exp(-distance * distance / (2.0 * 1.2 * 1.2))


def tap_matrix(cell_ids, anchors, offsets):
    span = TS - KTAPS + 1
    anchor_y = anchors // span
    anchor_x = anchors % span
    taps_y = kernel_taps(offsets // OSAMP)
    taps_x = kernel_taps(offsets % OSAMP)
    cell_y = cell_ids // TS
    cell_x = cell_ids % TS
    along_y = jnp.zeros((cell_ids.shape[0], anchors.shape[0]), jnp.float32)
    along_x = jnp.zeros((cell_ids.shape[0], anchors.shape[0]), jnp.float32)
    for step in range(KTAPS):
        along_y = along_y + jnp.where(
            cell_y[:, None] == anchor_y[None, :] + step, taps_y[None, :, step], 0.0
        )
        along_x = along_x + jnp.where(
            cell_x[:, None] == anchor_x[None, :] + step, taps_x[None, :, step], 0.0
        )
    return (along_y * along_x).astype(jnp.bfloat16)


def delay_table():
    freq = jnp.arange(NCH, dtype=jnp.int32)
    hi = jnp.arange(NCH // SPLIT, dtype=jnp.int32)
    lo = jnp.arange(SPLIT, dtype=jnp.int32)
    scale = 2.0 * math.pi / NCH
    ang_hi = scale * ((freq[:, None] * (SPLIT * hi)[None, :]) % NCH).astype(jnp.float32)
    ang_lo = scale * ((freq[:, None] * lo[None, :]) % NCH).astype(jnp.float32)
    c_hi, s_hi = jnp.cos(ang_hi), jnp.sin(ang_hi)
    c_lo, s_lo = jnp.cos(ang_lo), jnp.sin(ang_lo)
    cosine = c_hi[:, :, None] * c_lo[:, None, :] - s_hi[:, :, None] * s_lo[:, None, :]
    sine = s_hi[:, :, None] * c_lo[:, None, :] + c_hi[:, :, None] * s_lo[:, None, :]
    window_arg = 2.0 * math.pi * freq.astype(jnp.float32) / (NCH - 1)
    taper = (
        0.35875
        - 0.48829 * jnp.cos(window_arg)
        + 0.14128 * jnp.cos(2.0 * window_arg)
        - 0.01168 * jnp.cos(3.0 * window_arg)
    )
    tap_cos = (taper[:, None, None] * cosine).reshape(NCH, NCH)
    tap_sin = (taper[:, None, None] * sine).reshape(NCH, NCH)
    upper = jnp.concatenate([tap_cos, -tap_sin], axis=1)
    lower = jnp.concatenate([tap_sin, tap_cos], axis=1)
    return jnp.concatenate([upper, lower], axis=0).astype(jnp.bfloat16)


def halving_order(tm_index, time_groups, cell_share):
    level_bits = int(math.log2(time_groups))
    quarter = jnp.zeros((time_groups,), jnp.int32)
    for j in range(time_groups):
        value = tm_index
        pos = j
        for level in range(level_bits):
            half = time_groups >> (level + 1)
            sent = pos < half
            bit = 1 << level
            value = jnp.where(sent, value ^ bit, value)
            pos = pos % half if half > 0 else pos
        quarter = quarter.at[j].set(value)
    cells = quarter[:, None] * cell_share + jnp.arange(cell_share, dtype=jnp.int32)[None, :]
    return cells.reshape(-1)


def halving_reduce(partial, time_groups):
    level_bits = int(math.log2(time_groups))
    for level in range(level_bits):
        half = partial.shape[0] // 2
        bit = 1 << level
        perm = [(i, i ^ bit) for i in range(time_groups)]
        received = lax.ppermute(partial[:half], "tm", perm)
        partial = partial[half:] + received
    return partial


def per_device(visibility, anchor, offset, slot_rows, counts):
    time_groups = lax.axis_size("tm")
    cell_share = TS * TS // time_groups
    vis_rows = visibility[0]
    row_count, row_width = vis_rows.shape
    slot_table = slot_rows[0, 0]
    tile_count, slot_depth = slot_table.shape
    is_live = (jnp.arange(slot_depth, dtype=jnp.int32)[None, :] < counts[0, 0][:, None]).reshape(-1)
    flat_index = slot_table.reshape(-1)
    pick = (
        (flat_index[:, None] == jnp.arange(row_count, dtype=jnp.int32)[None, :]) & is_live[:, None]
    ).astype(jnp.bfloat16)
    meta_rows = jnp.concatenate(
        [
            anchor.astype(jnp.bfloat16),
            offset.astype(jnp.bfloat16),
            jnp.zeros((META - 2, row_count), jnp.bfloat16),
        ],
        axis=0,
    )
    meta = lax.dot_general(
        pick, meta_rows, (((1,), (1,)), ((), ())), preferred_element_type=jnp.float32
    ).astype(jnp.bfloat16)
    pow2 = time_groups & (time_groups - 1) == 0
    tm_index = lax.axis_index("tm")
    if pow2:
        cells = halving_order(tm_index, time_groups, cell_share)
    else:
        cells = jnp.arange(TS * TS, dtype=jnp.int32)
    transform = delay_table()
    width = row_width // CHUNKS
    weights = None
    total = None
    for chunk in range(CHUNKS):
        cols = slice(chunk * width, (chunk + 1) * width)
        picked = jnp.dot(pick, vis_rows[:, cols], preferred_element_type=jnp.float32)
        picked = picked.astype(jnp.bfloat16)
        if chunk == 0:
            picked = jnp.concatenate([picked, meta], axis=1)
        outgoing = picked.reshape(tile_count, slot_depth, picked.shape[1])
        arrived = lax.all_to_all(outgoing, "uv", split_axis=0, concat_axis=0, tiled=True)
        arrived = arrived.reshape(-1, picked.shape[1])
        if chunk == 0:
            arr_anchor = arrived[:, width].astype(jnp.int32)
            arr_offset = arrived[:, width + 1].astype(jnp.int32)
            weights = tap_matrix(cells, arr_anchor, arr_offset)
        partial = jnp.dot(weights, arrived[:, :width], preferred_element_type=jnp.float32)
        if pow2:
            summed = halving_reduce(partial, time_groups)
        else:
            summed = lax.psum_scatter(partial, "tm", scatter_dimension=0, tiled=True)
        grid = summed.astype(jnp.bfloat16)
        part = jnp.dot(grid, transform[cols], preferred_element_type=jnp.float32)
        total = part if total is None else total + part
    out_scale = 4.0 / math.sqrt(NCH * time_groups * ROWS_DEV)
    return total * out_scale


def solution(mesh):
    in_specs = (
        P("tm", "uv", None),
        P("tm", "uv"),
        P("tm", "uv"),
        P("tm", "uv", None, None),
        P("tm", "uv", None),
    )
    out_specs = P(("uv", "tm"), None)
    return jax.shard_map(
        per_device, mesh=mesh, in_specs=in_specs, out_specs=out_specs, check_vma=False
    )
```

```python
import math

import jax
import jax.numpy as jnp
from jax import lax
from jax.sharding import PartitionSpec as P

NCH = 1024
ROWS_DEV = 128
TS = 16
KTAPS = 8
OSAMP = 8
META = 128
SPLIT = 32


def kernel_taps(offsets):
    tap_index = jnp.arange(KTAPS, dtype=jnp.float32)
    sub_shift = (offsets.astype(jnp.float32) + 0.5) / OSAMP
    distance = tap_index[None, :] - (KTAPS / 2 - 1.0) - sub_shift[:, None]
    return jnp.exp(-distance * distance / (2.0 * 1.2 * 1.2))


def tap_matrix(cell_ids, anchors, offsets):
    span = TS - KTAPS + 1
    anchor_y = anchors // span
    anchor_x = anchors % span
    taps_y = kernel_taps(offsets // OSAMP)
    taps_x = kernel_taps(offsets % OSAMP)
    cell_y = cell_ids // TS
    cell_x = cell_ids % TS
    along_y = jnp.zeros((cell_ids.shape[0], anchors.shape[0]), jnp.float32)
    along_x = jnp.zeros((cell_ids.shape[0], anchors.shape[0]), jnp.float32)
    for step in range(KTAPS):
        along_y = along_y + jnp.where(
            cell_y[:, None] == anchor_y[None, :] + step, taps_y[None, :, step], 0.0
        )
        along_x = along_x + jnp.where(
            cell_x[:, None] == anchor_x[None, :] + step, taps_x[None, :, step], 0.0
        )
    return (along_y * along_x).astype(jnp.bfloat16)


def delay_halves():
    freq = jnp.arange(NCH, dtype=jnp.int32)
    hi = jnp.arange(NCH // SPLIT, dtype=jnp.int32)
    lo = jnp.arange(SPLIT, dtype=jnp.int32)
    scale = 2.0 * math.pi / NCH
    ang_hi = scale * ((freq[:, None] * (SPLIT * hi)[None, :]) % NCH).astype(jnp.float32)
    ang_lo = scale * ((freq[:, None] * lo[None, :]) % NCH).astype(jnp.float32)
    c_hi, s_hi = jnp.cos(ang_hi), jnp.sin(ang_hi)
    c_lo, s_lo = jnp.cos(ang_lo), jnp.sin(ang_lo)
    cosine = c_hi[:, :, None] * c_lo[:, None, :] - s_hi[:, :, None] * s_lo[:, None, :]
    sine = s_hi[:, :, None] * c_lo[:, None, :] + c_hi[:, :, None] * s_lo[:, None, :]
    window_arg = 2.0 * math.pi * freq.astype(jnp.float32) / (NCH - 1)
    taper = (
        0.35875
        - 0.48829 * jnp.cos(window_arg)
        + 0.14128 * jnp.cos(2.0 * window_arg)
        - 0.01168 * jnp.cos(3.0 * window_arg)
    )
    tap_cos = (taper[:, None, None] * cosine).reshape(NCH, NCH)
    tap_sin = (taper[:, None, None] * sine).reshape(NCH, NCH)
    return jnp.concatenate([tap_cos, tap_sin], axis=0).astype(jnp.bfloat16)


def halving_order(tm_index, time_groups, cell_share):
    level_bits = int(math.log2(time_groups))
    quarter = jnp.zeros((time_groups,), jnp.int32)
    for j in range(time_groups):
        value = tm_index
        pos = j
        for level in range(level_bits):
            half = time_groups >> (level + 1)
            sent = pos < half
            bit = 1 << level
            value = jnp.where(sent, value ^ bit, value)
            pos = pos % half if half > 0 else pos
        quarter = quarter.at[j].set(value)
    cells = quarter[:, None] * cell_share + jnp.arange(cell_share, dtype=jnp.int32)[None, :]
    return cells.reshape(-1)


def halving_reduce(partial, time_groups):
    level_bits = int(math.log2(time_groups))
    for level in range(level_bits):
        half = partial.shape[0] // 2
        bit = 1 << level
        perm = [(i, i ^ bit) for i in range(time_groups)]
        received = lax.ppermute(partial[:half], "tm", perm)
        partial = partial[half:] + received
    return partial


def uv_exchange(outgoing, uv_size):
    if uv_size > 16:
        return lax.all_to_all(outgoing, "uv", split_axis=0, concat_axis=0, tiled=True)
    pieces = [outgoing[0]]
    for shift in range(1, uv_size):
        perm = [(i, (i + shift) % uv_size) for i in range(uv_size)]
        pieces.append(lax.ppermute(outgoing[shift], "uv", perm))
    return jnp.stack(pieces)


def per_device(visibility, anchor, offset, slot_rows, counts):
    time_groups = lax.axis_size("tm")
    uv_size = lax.axis_size("uv")
    cell_share = TS * TS // time_groups
    vis_rows = visibility[0]
    row_count, row_width = vis_rows.shape
    slot_table = slot_rows[0, 0]
    live_count = counts[0, 0]
    tile_count, slot_depth = slot_table.shape
    if uv_size <= 16:
        rotate = (lax.axis_index("uv") + jnp.arange(tile_count, dtype=jnp.int32)) % tile_count
        slot_table = jnp.take(slot_table, rotate, axis=0)
        live_count = jnp.take(live_count, rotate)
    is_live = (jnp.arange(slot_depth, dtype=jnp.int32)[None, :] < live_count[:, None]).reshape(-1)
    flat_index = slot_table.reshape(-1)
    pick = (
        (flat_index[:, None] == jnp.arange(row_count, dtype=jnp.int32)[None, :]) & is_live[:, None]
    ).astype(jnp.bfloat16)
    picked = jnp.dot(pick, vis_rows, preferred_element_type=jnp.float32).astype(jnp.bfloat16)
    meta_rows = jnp.concatenate(
        [
            anchor.astype(jnp.bfloat16),
            offset.astype(jnp.bfloat16),
            jnp.zeros((META - 2, row_count), jnp.bfloat16),
        ],
        axis=0,
    )
    meta = lax.dot_general(
        pick, meta_rows, (((1,), (1,)), ((), ())), preferred_element_type=jnp.float32
    ).astype(jnp.bfloat16)
    outgoing = jnp.concatenate([picked, meta], axis=1).reshape(tile_count, slot_depth, row_width + META)
    arrived = uv_exchange(outgoing, uv_size)
    arrived = arrived.reshape(-1, row_width + META)
    arr_anchor = arrived[:, row_width].astype(jnp.int32)
    arr_offset = arrived[:, row_width + 1].astype(jnp.int32)
    tm_index = lax.axis_index("tm")
    pow2 = time_groups & (time_groups - 1) == 0
    if pow2:
        cells = halving_order(tm_index, time_groups, cell_share)
    else:
        cells = jnp.arange(TS * TS, dtype=jnp.int32)
    weights = tap_matrix(cells, arr_anchor, arr_offset)
    partial = jnp.dot(weights, arrived[:, :row_width], preferred_element_type=jnp.float32)
    if pow2:
        summed = halving_reduce(partial, time_groups)
    else:
        summed = lax.psum_scatter(partial, "tm", scatter_dimension=0, tiled=True)
    grid = summed.astype(jnp.bfloat16)
    grid_re, grid_im = grid[:, :NCH], grid[:, NCH:]
    lhs = jnp.concatenate(
        [grid, jnp.concatenate([grid_im, -grid_re], axis=1)], axis=0
    )
    out_scale = 4.0 / math.sqrt(NCH * time_groups * ROWS_DEV)
    both = jnp.dot(lhs, delay_halves(), preferred_element_type=jnp.float32) * out_scale
    cells_out = grid.shape[0]
    return jnp.concatenate([both[:cells_out], both[cells_out:]], axis=1)


def solution(mesh):
    in_specs = (
        P("tm", "uv", None),
        P("tm", "uv"),
        P("tm", "uv"),
        P("tm", "uv", None, None),
        P("tm", "uv", None),
    )
    out_specs = P(("uv", "tm"), None)
    return jax.shard_map(
        per_device, mesh=mesh, in_specs=in_specs, out_specs=out_specs, check_vma=False
    )
```

```python
import math

import jax
import jax.numpy as jnp
from jax import lax
from jax.sharding import PartitionSpec as P

NCH = 1024
ROWS_DEV = 128
TS = 16
KTAPS = 8
OSAMP = 8
META = 128
SPLIT = 32


def kernel_taps(offsets):
    tap_index = jnp.arange(KTAPS, dtype=jnp.float32)
    sub_shift = (offsets.astype(jnp.float32) + 0.5) / OSAMP
    distance = tap_index[None, :] - (KTAPS / 2 - 1.0) - sub_shift[:, None]
    return jnp.exp(-distance * distance / (2.0 * 1.2 * 1.2))


def tap_matrix(cell_ids, anchors, offsets):
    span = TS - KTAPS + 1
    anchor_y = anchors // span
    anchor_x = anchors % span
    taps_y = kernel_taps(offsets // OSAMP)
    taps_x = kernel_taps(offsets % OSAMP)
    cell_y = cell_ids // TS
    cell_x = cell_ids % TS
    along_y = jnp.zeros((cell_ids.shape[0], anchors.shape[0]), jnp.float32)
    along_x = jnp.zeros((cell_ids.shape[0], anchors.shape[0]), jnp.float32)
    for step in range(KTAPS):
        along_y = along_y + jnp.where(
            cell_y[:, None] == anchor_y[None, :] + step, taps_y[None, :, step], 0.0
        )
        along_x = along_x + jnp.where(
            cell_x[:, None] == anchor_x[None, :] + step, taps_x[None, :, step], 0.0
        )
    return (along_y * along_x).astype(jnp.bfloat16)


def delay_halves():
    freq = jnp.arange(NCH, dtype=jnp.int32)
    hi = jnp.arange(NCH // SPLIT, dtype=jnp.int32)
    lo = jnp.arange(SPLIT, dtype=jnp.int32)
    scale = 2.0 * math.pi / NCH
    ang_hi = scale * ((freq[:, None] * (SPLIT * hi)[None, :]) % NCH).astype(jnp.float32)
    ang_lo = scale * ((freq[:, None] * lo[None, :]) % NCH).astype(jnp.float32)
    c_hi, s_hi = jnp.cos(ang_hi), jnp.sin(ang_hi)
    c_lo, s_lo = jnp.cos(ang_lo), jnp.sin(ang_lo)
    cosine = c_hi[:, :, None] * c_lo[:, None, :] - s_hi[:, :, None] * s_lo[:, None, :]
    sine = s_hi[:, :, None] * c_lo[:, None, :] + c_hi[:, :, None] * s_lo[:, None, :]
    window_arg = 2.0 * math.pi * freq.astype(jnp.float32) / (NCH - 1)
    taper = (
        0.35875
        - 0.48829 * jnp.cos(window_arg)
        + 0.14128 * jnp.cos(2.0 * window_arg)
        - 0.01168 * jnp.cos(3.0 * window_arg)
    )
    tap_cos = (taper[:, None, None] * cosine).reshape(NCH, NCH)
    tap_sin = (taper[:, None, None] * sine).reshape(NCH, NCH)
    return jnp.concatenate([tap_cos, tap_sin], axis=0).astype(jnp.bfloat16)


def halving_order(tm_index, time_groups, cell_share):
    level_bits = int(math.log2(time_groups))
    quarter = jnp.zeros((time_groups,), jnp.int32)
    for j in range(time_groups):
        value = tm_index
        pos = j
        for level in range(level_bits):
            half = time_groups >> (level + 1)
            sent = pos < half
            bit = 1 << level
            value = jnp.where(sent, value ^ bit, value)
            pos = pos % half if half > 0 else pos
        quarter = quarter.at[j].set(value)
    cells = quarter[:, None] * cell_share + jnp.arange(cell_share, dtype=jnp.int32)[None, :]
    return cells.reshape(-1)


def halving_reduce(partial, time_groups):
    level_bits = int(math.log2(time_groups))
    for level in range(level_bits):
        half = partial.shape[0] // 2
        bit = 1 << level
        perm = [(i, i ^ bit) for i in range(time_groups)]
        outgoing = partial[:half]
        if level > 0:
            outgoing = outgoing.astype(jnp.bfloat16)
        received = lax.ppermute(outgoing, "tm", perm)
        partial = partial[half:] + received.astype(jnp.float32)
    return partial


def uv_exchange(outgoing, uv_size):
    if uv_size > 16:
        return lax.all_to_all(outgoing, "uv", split_axis=0, concat_axis=0, tiled=True)
    pieces = [outgoing[0]]
    for shift in range(1, uv_size):
        perm = [(i, (i + shift) % uv_size) for i in range(uv_size)]
        pieces.append(lax.ppermute(outgoing[shift], "uv", perm))
    return jnp.stack(pieces)


def per_device(visibility, anchor, offset, slot_rows, counts):
    time_groups = lax.axis_size("tm")
    uv_size = lax.axis_size("uv")
    cell_share = TS * TS // time_groups
    vis_rows = visibility[0]
    row_count, row_width = vis_rows.shape
    slot_table = slot_rows[0, 0]
    live_count = counts[0, 0]
    tile_count, slot_depth = slot_table.shape
    if uv_size <= 16:
        uv_index = lax.axis_index("uv")
        slot_table = lax.dynamic_slice_in_dim(
            jnp.concatenate([slot_table, slot_table], axis=0), uv_index, tile_count, 0
        )
        live_count = lax.dynamic_slice_in_dim(
            jnp.concatenate([live_count, live_count], axis=0), uv_index, tile_count, 0
        )
    is_live = (jnp.arange(slot_depth, dtype=jnp.int32)[None, :] < live_count[:, None]).reshape(-1)
    flat_index = slot_table.reshape(-1)
    pick = (
        (flat_index[:, None] == jnp.arange(row_count, dtype=jnp.int32)[None, :]) & is_live[:, None]
    ).astype(jnp.bfloat16)
    picked = jnp.dot(pick, vis_rows, preferred_element_type=jnp.float32).astype(jnp.bfloat16)
    meta_rows = jnp.concatenate(
        [anchor, offset, jnp.zeros((META - 2, row_count), jnp.int32)], axis=0
    ).astype(jnp.bfloat16)
    meta = lax.dot_general(
        pick, meta_rows, (((1,), (1,)), ((), ())), preferred_element_type=jnp.float32
    ).astype(jnp.bfloat16)
    outgoing = jnp.concatenate([picked, meta], axis=1).reshape(tile_count, slot_depth, row_width + META)
    arrived = uv_exchange(outgoing, uv_size)
    arrived = arrived.reshape(-1, row_width + META)
    arr_anchor = arrived[:, row_width].astype(jnp.int32)
    arr_offset = arrived[:, row_width + 1].astype(jnp.int32)
    tm_index = lax.axis_index("tm")
    pow2 = time_groups & (time_groups - 1) == 0
    if pow2:
        cells = halving_order(tm_index, time_groups, cell_share)
    else:
        cells = jnp.arange(TS * TS, dtype=jnp.int32)
    weights = tap_matrix(cells, arr_anchor, arr_offset)
    partial = jnp.dot(weights, arrived[:, :row_width], preferred_element_type=jnp.float32)
    if pow2:
        summed = halving_reduce(partial, time_groups)
    else:
        summed = lax.psum_scatter(partial, "tm", scatter_dimension=0, tiled=True)
    grid = summed.astype(jnp.bfloat16)
    grid_re, grid_im = grid[:, :NCH], grid[:, NCH:]
    lhs = jnp.concatenate(
        [grid, jnp.concatenate([grid_im, -grid_re], axis=1)], axis=0
    )
    out_scale = 4.0 / math.sqrt(NCH * time_groups * ROWS_DEV)
    both = jnp.dot(lhs, delay_halves(), preferred_element_type=jnp.float32) * out_scale
    cells_out = grid.shape[0]
    return jnp.concatenate([both[:cells_out], both[cells_out:]], axis=1)


def solution(mesh):
    in_specs = (
        P("tm", "uv", None),
        P("tm", "uv"),
        P("tm", "uv"),
        P("tm", "uv", None, None),
        P("tm", "uv", None),
    )
    out_specs = P(("uv", "tm"), None)
    return jax.shard_map(
        per_device, mesh=mesh, in_specs=in_specs, out_specs=out_specs, check_vma=False
    )
```

```python
import math

import jax
import jax.numpy as jnp
from jax import lax
from jax.sharding import PartitionSpec as P

NCH = 1024
ROWS_DEV = 128
TS = 16
KTAPS = 8
OSAMP = 8
META = 128
SPLIT = 32
CHUNKS = 2


def kernel_taps(offsets):
    tap_index = jnp.arange(KTAPS, dtype=jnp.float32)
    sub_shift = (offsets.astype(jnp.float32) + 0.5) / OSAMP
    distance = tap_index[None, :] - (KTAPS / 2 - 1.0) - sub_shift[:, None]
    return jnp.exp(-distance * distance / (2.0 * 1.2 * 1.2))


def tap_matrix(cell_ids, anchors, offsets):
    span = TS - KTAPS + 1
    anchor_y = anchors // span
    anchor_x = anchors % span
    taps_y = kernel_taps(offsets // OSAMP)
    taps_x = kernel_taps(offsets % OSAMP)
    cell_y = cell_ids // TS
    cell_x = cell_ids % TS
    along_y = jnp.zeros((cell_ids.shape[0], anchors.shape[0]), jnp.float32)
    along_x = jnp.zeros((cell_ids.shape[0], anchors.shape[0]), jnp.float32)
    for step in range(KTAPS):
        along_y = along_y + jnp.where(
            cell_y[:, None] == anchor_y[None, :] + step, taps_y[None, :, step], 0.0
        )
        along_x = along_x + jnp.where(
            cell_x[:, None] == anchor_x[None, :] + step, taps_x[None, :, step], 0.0
        )
    return (along_y * along_x).astype(jnp.bfloat16)


def delay_halves():
    freq = jnp.arange(NCH, dtype=jnp.int32)
    hi = jnp.arange(NCH // SPLIT, dtype=jnp.int32)
    lo = jnp.arange(SPLIT, dtype=jnp.int32)
    scale = 2.0 * math.pi / NCH
    ang_hi = scale * ((freq[:, None] * (SPLIT * hi)[None, :]) % NCH).astype(jnp.float32)
    ang_lo = scale * ((freq[:, None] * lo[None, :]) % NCH).astype(jnp.float32)
    c_hi, s_hi = jnp.cos(ang_hi), jnp.sin(ang_hi)
    c_lo, s_lo = jnp.cos(ang_lo), jnp.sin(ang_lo)
    cosine = c_hi[:, :, None] * c_lo[:, None, :] - s_hi[:, :, None] * s_lo[:, None, :]
    sine = s_hi[:, :, None] * c_lo[:, None, :] + c_hi[:, :, None] * s_lo[:, None, :]
    window_arg = 2.0 * math.pi * freq.astype(jnp.float32) / (NCH - 1)
    taper = (
        0.35875
        - 0.48829 * jnp.cos(window_arg)
        + 0.14128 * jnp.cos(2.0 * window_arg)
        - 0.01168 * jnp.cos(3.0 * window_arg)
    )
    tap_cos = (taper[:, None, None] * cosine).reshape(NCH, NCH)
    tap_sin = (taper[:, None, None] * sine).reshape(NCH, NCH)
    return jnp.concatenate([tap_cos, tap_sin], axis=0).astype(jnp.bfloat16)


def full_table():
    halves = delay_halves()
    tap_cos, tap_sin = halves[:NCH], halves[NCH:]
    upper = jnp.concatenate([tap_cos, -tap_sin], axis=1)
    lower = jnp.concatenate([tap_sin, tap_cos], axis=1)
    return jnp.concatenate([upper, lower], axis=0)


def halving_order(tm_index, time_groups, cell_share):
    level_bits = int(math.log2(time_groups))
    quarter = jnp.zeros((time_groups,), jnp.int32)
    for j in range(time_groups):
        value = tm_index
        pos = j
        for level in range(level_bits):
            half = time_groups >> (level + 1)
            sent = pos < half
            bit = 1 << level
            value = jnp.where(sent, value ^ bit, value)
            pos = pos % half if half > 0 else pos
        quarter = quarter.at[j].set(value)
    cells = quarter[:, None] * cell_share + jnp.arange(cell_share, dtype=jnp.int32)[None, :]
    return cells.reshape(-1)


def halving_send(partial, level, time_groups):
    half = partial.shape[0] // 2
    bit = 1 << level
    perm = [(i, i ^ bit) for i in range(time_groups)]
    outgoing = partial[:half]
    if level > 0:
        outgoing = outgoing.astype(jnp.bfloat16)
    return partial[half:], lax.ppermute(outgoing, "tm", perm)


def halving_reduce(partial, time_groups):
    level_bits = int(math.log2(time_groups))
    for level in range(level_bits):
        half = partial.shape[0] // 2
        bit = 1 << level
        perm = [(i, i ^ bit) for i in range(time_groups)]
        outgoing = partial[:half]
        if level > 0:
            outgoing = outgoing.astype(jnp.bfloat16)
        received = lax.ppermute(outgoing, "tm", perm)
        partial = partial[half:] + received.astype(jnp.float32)
    return partial


def uv_exchange(outgoing, uv_size):
    if uv_size > 16:
        return lax.all_to_all(outgoing, "uv", split_axis=0, concat_axis=0, tiled=True)
    pieces = [outgoing[0]]
    for shift in range(1, uv_size):
        perm = [(i, (i + shift) % uv_size) for i in range(uv_size)]
        pieces.append(lax.ppermute(outgoing[shift], "uv", perm))
    return jnp.stack(pieces)


def per_device(visibility, anchor, offset, slot_rows, counts):
    time_groups = lax.axis_size("tm")
    uv_size = lax.axis_size("uv")
    cell_share = TS * TS // time_groups
    vis_rows = visibility[0]
    row_count, row_width = vis_rows.shape
    slot_table = slot_rows[0, 0]
    live_count = counts[0, 0]
    tile_count, slot_depth = slot_table.shape
    if uv_size <= 16:
        uv_index = lax.axis_index("uv")
        slot_table = lax.dynamic_slice_in_dim(
            jnp.concatenate([slot_table, slot_table], axis=0), uv_index, tile_count, 0
        )
        live_count = lax.dynamic_slice_in_dim(
            jnp.concatenate([live_count, live_count], axis=0), uv_index, tile_count, 0
        )
    is_live = (jnp.arange(slot_depth, dtype=jnp.int32)[None, :] < live_count[:, None]).reshape(-1)
    flat_index = slot_table.reshape(-1)
    pick = (
        (flat_index[:, None] == jnp.arange(row_count, dtype=jnp.int32)[None, :]) & is_live[:, None]
    ).astype(jnp.bfloat16)
    picked = jnp.dot(pick, vis_rows, preferred_element_type=jnp.float32).astype(jnp.bfloat16)
    meta_rows = jnp.concatenate(
        [anchor, offset, jnp.zeros((META - 2, row_count), jnp.int32)], axis=0
    ).astype(jnp.bfloat16)
    meta = lax.dot_general(
        pick, meta_rows, (((1,), (1,)), ((), ())), preferred_element_type=jnp.float32
    ).astype(jnp.bfloat16)
    tm_index = lax.axis_index("tm")
    pow2 = time_groups & (time_groups - 1) == 0
    if pow2:
        cells = halving_order(tm_index, time_groups, cell_share)
    else:
        cells = jnp.arange(TS * TS, dtype=jnp.int32)
    transform = full_table()
    width = row_width // CHUNKS
    total = None
    weights = None
    partial = None
    for chunk in range(CHUNKS):
        cols = slice(chunk * width, (chunk + 1) * width)
        piece = picked[:, cols]
        if chunk == 0:
            piece = jnp.concatenate([piece, meta], axis=1)
        elif pow2:
            levels = int(math.log2(time_groups))
            for level in range(levels - 1):
                kept, received = halving_send(partial, level, time_groups)
                partial = kept + received.astype(jnp.float32)
            partial, piece = lax.optimization_barrier((partial, piece))
            kept, received = halving_send(partial, levels - 1, time_groups)
        outgoing = piece.reshape(tile_count, slot_depth, piece.shape[1])
        arrived = uv_exchange(outgoing, uv_size).reshape(-1, piece.shape[1])
        if chunk > 0:
            if pow2:
                received, arrived = lax.optimization_barrier((received, arrived))
                summed = kept + received.astype(jnp.float32)
            else:
                summed = lax.psum_scatter(partial, "tm", scatter_dimension=0, tiled=True)
            grid = summed.astype(jnp.bfloat16)
            prev = slice((chunk - 1) * width, chunk * width)
            part = jnp.dot(grid, transform[prev], preferred_element_type=jnp.float32)
            total = part if total is None else total + part
        if chunk == 0:
            arr_anchor = arrived[:, width].astype(jnp.int32)
            arr_offset = arrived[:, width + 1].astype(jnp.int32)
            weights = tap_matrix(cells, arr_anchor, arr_offset)
        partial = jnp.dot(weights, arrived[:, :width], preferred_element_type=jnp.float32)
    if pow2:
        summed = halving_reduce(partial, time_groups)
    else:
        summed = lax.psum_scatter(partial, "tm", scatter_dimension=0, tiled=True)
    grid = summed.astype(jnp.bfloat16)
    part = jnp.dot(grid, transform[cols], preferred_element_type=jnp.float32)
    total = part if total is None else total + part
    out_scale = 4.0 / math.sqrt(NCH * time_groups * ROWS_DEV)
    return total * out_scale


def solution(mesh):
    in_specs = (
        P("tm", "uv", None),
        P("tm", "uv"),
        P("tm", "uv"),
        P("tm", "uv", None, None),
        P("tm", "uv", None),
    )
    out_specs = P(("uv", "tm"), None)
    return jax.shard_map(
        per_device, mesh=mesh, in_specs=in_specs, out_specs=out_specs, check_vma=False
    )
```

```python
import math

import jax
import jax.numpy as jnp
from jax import lax
from jax.sharding import PartitionSpec as P

NCH = 1024
ROWS_DEV = 128
TS = 16
KTAPS = 8
OSAMP = 8
META = 128
SPLIT = 32


def kernel_taps(offsets):
    tap_index = jnp.arange(KTAPS, dtype=jnp.float32)
    sub_shift = (offsets.astype(jnp.float32) + 0.5) / OSAMP
    distance = tap_index[None, :] - (KTAPS / 2 - 1.0) - sub_shift[:, None]
    return jnp.exp(-distance * distance / (2.0 * 1.2 * 1.2))


def tap_matrix(cell_ids, anchors, offsets):
    span = TS - KTAPS + 1
    anchor_y = anchors // span
    anchor_x = anchors % span
    taps_y = kernel_taps(offsets // OSAMP)
    taps_x = kernel_taps(offsets % OSAMP)
    cell_y = cell_ids // TS
    cell_x = cell_ids % TS
    along_y = jnp.zeros((cell_ids.shape[0], anchors.shape[0]), jnp.float32)
    along_x = jnp.zeros((cell_ids.shape[0], anchors.shape[0]), jnp.float32)
    for step in range(KTAPS):
        along_y = along_y + jnp.where(
            cell_y[:, None] == anchor_y[None, :] + step, taps_y[None, :, step], 0.0
        )
        along_x = along_x + jnp.where(
            cell_x[:, None] == anchor_x[None, :] + step, taps_x[None, :, step], 0.0
        )
    return (along_y * along_x).astype(jnp.bfloat16)


def delay_halves():
    freq = jnp.arange(NCH, dtype=jnp.int32)
    hi = jnp.arange(NCH // SPLIT, dtype=jnp.int32)
    lo = jnp.arange(SPLIT, dtype=jnp.int32)
    scale = 2.0 * math.pi / NCH
    ang_hi = scale * ((freq[:, None] * (SPLIT * hi)[None, :]) % NCH).astype(jnp.float32)
    ang_lo = scale * ((freq[:, None] * lo[None, :]) % NCH).astype(jnp.float32)
    c_hi, s_hi = jnp.cos(ang_hi), jnp.sin(ang_hi)
    c_lo, s_lo = jnp.cos(ang_lo), jnp.sin(ang_lo)
    cosine = c_hi[:, :, None] * c_lo[:, None, :] - s_hi[:, :, None] * s_lo[:, None, :]
    sine = s_hi[:, :, None] * c_lo[:, None, :] + c_hi[:, :, None] * s_lo[:, None, :]
    window_arg = 2.0 * math.pi * freq.astype(jnp.float32) / (NCH - 1)
    taper = (
        0.35875
        - 0.48829 * jnp.cos(window_arg)
        + 0.14128 * jnp.cos(2.0 * window_arg)
        - 0.01168 * jnp.cos(3.0 * window_arg)
    )
    tap_cos = (taper[:, None, None] * cosine).reshape(NCH, NCH)
    tap_sin = (taper[:, None, None] * sine).reshape(NCH, NCH)
    return jnp.concatenate([tap_cos, tap_sin], axis=0).astype(jnp.bfloat16)


def full_table():
    halves = delay_halves()
    tap_cos, tap_sin = halves[:NCH], halves[NCH:]
    upper = jnp.concatenate([tap_cos, -tap_sin], axis=1)
    lower = jnp.concatenate([tap_sin, tap_cos], axis=1)
    return jnp.concatenate([upper, lower], axis=0)


def halving_order(tm_index, time_groups, cell_share):
    level_bits = int(math.log2(time_groups))
    quarter = jnp.zeros((time_groups,), jnp.int32)
    for j in range(time_groups):
        value = tm_index
        pos = j
        for level in range(level_bits):
            half = time_groups >> (level + 1)
            sent = pos < half
            bit = 1 << level
            value = jnp.where(sent, value ^ bit, value)
            pos = pos % half if half > 0 else pos
        quarter = quarter.at[j].set(value)
    cells = quarter[:, None] * cell_share + jnp.arange(cell_share, dtype=jnp.int32)[None, :]
    return cells.reshape(-1)


def halving_reduce(partial, time_groups):
    level_bits = int(math.log2(time_groups))
    for level in range(level_bits):
        half = partial.shape[0] // 2
        bit = 1 << level
        perm = [(i, i ^ bit) for i in range(time_groups)]
        outgoing = partial[:half]
        if level > 0:
            outgoing = outgoing.astype(jnp.bfloat16)
        received = lax.ppermute(outgoing, "tm", perm)
        partial = partial[half:] + received.astype(jnp.float32)
    return partial


def uv_exchange(outgoing, uv_size):
    if uv_size > 16:
        return lax.all_to_all(outgoing, "uv", split_axis=0, concat_axis=0, tiled=True)
    pieces = [outgoing[0]]
    for shift in range(1, uv_size):
        perm = [(i, (i + shift) % uv_size) for i in range(uv_size)]
        pieces.append(lax.ppermute(outgoing[shift], "uv", perm))
    return jnp.stack(pieces)


def per_device(visibility, anchor, offset, slot_rows, counts):
    time_groups = lax.axis_size("tm")
    uv_size = lax.axis_size("uv")
    cell_share = TS * TS // time_groups
    vis_rows = visibility[0]
    row_count, row_width = vis_rows.shape
    slot_table = slot_rows[0, 0]
    live_count = counts[0, 0]
    tile_count, slot_depth = slot_table.shape
    if uv_size <= 16:
        uv_index = lax.axis_index("uv")
        slot_table = lax.dynamic_slice_in_dim(
            jnp.concatenate([slot_table, slot_table], axis=0), uv_index, tile_count, 0
        )
        live_count = lax.dynamic_slice_in_dim(
            jnp.concatenate([live_count, live_count], axis=0), uv_index, tile_count, 0
        )
    is_live = (jnp.arange(slot_depth, dtype=jnp.int32)[None, :] < live_count[:, None]).reshape(-1)
    flat_index = slot_table.reshape(-1)
    pick = (
        (flat_index[:, None] == jnp.arange(row_count, dtype=jnp.int32)[None, :]) & is_live[:, None]
    ).astype(jnp.bfloat16)
    picked = jnp.dot(pick, vis_rows, preferred_element_type=jnp.float32).astype(jnp.bfloat16)
    meta_rows = jnp.concatenate(
        [anchor, offset, jnp.zeros((META - 2, row_count), jnp.int32)], axis=0
    ).astype(jnp.bfloat16)
    meta = lax.dot_general(
        pick, meta_rows, (((1,), (1,)), ((), ())), preferred_element_type=jnp.float32
    ).astype(jnp.bfloat16)
    outgoing = jnp.concatenate([picked, meta], axis=1).reshape(tile_count, slot_depth, row_width + META)
    transform = full_table()
    arrived = uv_exchange(outgoing, uv_size)
    transform, arrived = lax.optimization_barrier((transform, arrived))
    arrived = arrived.reshape(-1, row_width + META)
    arr_anchor = arrived[:, row_width].astype(jnp.int32)
    arr_offset = arrived[:, row_width + 1].astype(jnp.int32)
    tm_index = lax.axis_index("tm")
    pow2 = time_groups & (time_groups - 1) == 0
    if pow2:
        cells = halving_order(tm_index, time_groups, cell_share)
    else:
        cells = jnp.arange(TS * TS, dtype=jnp.int32)
    weights = tap_matrix(cells, arr_anchor, arr_offset)
    partial = jnp.dot(weights, arrived[:, :row_width], preferred_element_type=jnp.float32)
    if pow2:
        summed = halving_reduce(partial, time_groups)
    else:
        summed = lax.psum_scatter(partial, "tm", scatter_dimension=0, tiled=True)
    grid = summed.astype(jnp.bfloat16)
    out_scale = 4.0 / math.sqrt(NCH * time_groups * ROWS_DEV)
    return jnp.dot(grid, transform, preferred_element_type=jnp.float32) * out_scale


def solution(mesh):
    in_specs = (
        P("tm", "uv", None),
        P("tm", "uv"),
        P("tm", "uv"),
        P("tm", "uv", None, None),
        P("tm", "uv", None),
    )
    out_specs = P(("uv", "tm"), None)
    return jax.shard_map(
        per_device, mesh=mesh, in_specs=in_specs, out_specs=out_specs, check_vma=False
    )
```

```python
import math

import jax
import jax.numpy as jnp
from jax import lax
from jax.sharding import PartitionSpec as P

NCH = 1024
ROWS_DEV = 128
TS = 16
KTAPS = 8
OSAMP = 8
META = 128
SPLIT = 32


def kernel_taps(offsets):
    tap_index = jnp.arange(KTAPS, dtype=jnp.float32)
    sub_shift = (offsets.astype(jnp.float32) + 0.5) / OSAMP
    distance = tap_index[None, :] - (KTAPS / 2 - 1.0) - sub_shift[:, None]
    return jnp.exp(-distance * distance / (2.0 * 1.2 * 1.2))


def tap_matrix(cell_ids, anchors, offsets):
    span = TS - KTAPS + 1
    anchor_y = anchors // span
    anchor_x = anchors % span
    taps_y = kernel_taps(offsets // OSAMP)
    taps_x = kernel_taps(offsets % OSAMP)
    cell_y = cell_ids // TS
    cell_x = cell_ids % TS
    along_y = jnp.zeros((cell_ids.shape[0], anchors.shape[0]), jnp.float32)
    along_x = jnp.zeros((cell_ids.shape[0], anchors.shape[0]), jnp.float32)
    for step in range(KTAPS):
        along_y = along_y + jnp.where(
            cell_y[:, None] == anchor_y[None, :] + step, taps_y[None, :, step], 0.0
        )
        along_x = along_x + jnp.where(
            cell_x[:, None] == anchor_x[None, :] + step, taps_x[None, :, step], 0.0
        )
    return (along_y * along_x).astype(jnp.bfloat16)


def delay_halves():
    freq = jnp.arange(NCH, dtype=jnp.int32)
    hi = jnp.arange(NCH // SPLIT, dtype=jnp.int32)
    lo = jnp.arange(SPLIT, dtype=jnp.int32)
    scale = 2.0 * math.pi / NCH
    ang_hi = scale * ((freq[:, None] * (SPLIT * hi)[None, :]) % NCH).astype(jnp.float32)
    ang_lo = scale * ((freq[:, None] * lo[None, :]) % NCH).astype(jnp.float32)
    c_hi, s_hi = jnp.cos(ang_hi), jnp.sin(ang_hi)
    c_lo, s_lo = jnp.cos(ang_lo), jnp.sin(ang_lo)
    cosine = c_hi[:, :, None] * c_lo[:, None, :] - s_hi[:, :, None] * s_lo[:, None, :]
    sine = s_hi[:, :, None] * c_lo[:, None, :] + c_hi[:, :, None] * s_lo[:, None, :]
    window_arg = 2.0 * math.pi * freq.astype(jnp.float32) / (NCH - 1)
    taper = (
        0.35875
        - 0.48829 * jnp.cos(window_arg)
        + 0.14128 * jnp.cos(2.0 * window_arg)
        - 0.01168 * jnp.cos(3.0 * window_arg)
    )
    tap_cos = (taper[:, None, None] * cosine).reshape(NCH, NCH)
    tap_sin = (taper[:, None, None] * sine).reshape(NCH, NCH)
    return tap_cos.astype(jnp.bfloat16), tap_sin.astype(jnp.bfloat16)


def halving_order(tm_index, time_groups, cell_share):
    level_bits = int(math.log2(time_groups))
    quarter = jnp.zeros((time_groups,), jnp.int32)
    for j in range(time_groups):
        value = tm_index
        pos = j
        for level in range(level_bits):
            half = time_groups >> (level + 1)
            sent = pos < half
            bit = 1 << level
            value = jnp.where(sent, value ^ bit, value)
            pos = pos % half if half > 0 else pos
        quarter = quarter.at[j].set(value)
    cells = quarter[:, None] * cell_share + jnp.arange(cell_share, dtype=jnp.int32)[None, :]
    return cells.reshape(-1)


def halving_reduce(partial, time_groups):
    level_bits = int(math.log2(time_groups))
    for level in range(level_bits):
        half = partial.shape[0] // 2
        bit = 1 << level
        perm = [(i, i ^ bit) for i in range(time_groups)]
        outgoing = partial[:half]
        if level > 0:
            outgoing = outgoing.astype(jnp.bfloat16)
        received = lax.ppermute(outgoing, "tm", perm)
        partial = partial[half:] + received.astype(jnp.float32)
    return partial


def uv_exchange(outgoing, uv_size):
    if uv_size > 16:
        return lax.all_to_all(outgoing, "uv", split_axis=0, concat_axis=0, tiled=True)
    pieces = [outgoing[0]]
    for shift in range(1, uv_size):
        perm = [(i, (i + shift) % uv_size) for i in range(uv_size)]
        pieces.append(lax.ppermute(outgoing[shift], "uv", perm))
    return jnp.stack(pieces)


def per_device(visibility, anchor, offset, slot_rows, counts):
    time_groups = lax.axis_size("tm")
    uv_size = lax.axis_size("uv")
    cell_share = TS * TS // time_groups
    vis_rows = visibility[0]
    row_count, row_width = vis_rows.shape
    slot_table = slot_rows[0, 0]
    live_count = counts[0, 0]
    tile_count, slot_depth = slot_table.shape
    if uv_size <= 16:
        uv_index = lax.axis_index("uv")
        slot_table = lax.dynamic_slice_in_dim(
            jnp.concatenate([slot_table, slot_table], axis=0), uv_index, tile_count, 0
        )
        live_count = lax.dynamic_slice_in_dim(
            jnp.concatenate([live_count, live_count], axis=0), uv_index, tile_count, 0
        )
    is_live = (jnp.arange(slot_depth, dtype=jnp.int32)[None, :] < live_count[:, None]).reshape(-1)
    flat_index = slot_table.reshape(-1)
    pick = (
        (flat_index[:, None] == jnp.arange(row_count, dtype=jnp.int32)[None, :]) & is_live[:, None]
    ).astype(jnp.bfloat16)
    picked = jnp.dot(pick, vis_rows, preferred_element_type=jnp.float32).astype(jnp.bfloat16)
    meta_rows = jnp.concatenate(
        [anchor, offset, jnp.zeros((META - 2, row_count), jnp.int32)], axis=0
    ).astype(jnp.bfloat16)
    meta = lax.dot_general(
        pick, meta_rows, (((1,), (1,)), ((), ())), preferred_element_type=jnp.float32
    ).astype(jnp.bfloat16)
    outgoing = jnp.concatenate([picked, meta], axis=1).reshape(tile_count, slot_depth, row_width + META)
    arrived = uv_exchange(outgoing, uv_size)
    (tap_cos, tap_sin), arrived = lax.optimization_barrier((delay_halves(), arrived))
    arrived = arrived.reshape(-1, row_width + META)
    arr_anchor = arrived[:, row_width].astype(jnp.int32)
    arr_offset = arrived[:, row_width + 1].astype(jnp.int32)
    tm_index = lax.axis_index("tm")
    pow2 = time_groups & (time_groups - 1) == 0
    if pow2:
        cells = halving_order(tm_index, time_groups, cell_share)
    else:
        cells = jnp.arange(TS * TS, dtype=jnp.int32)
    weights = tap_matrix(cells, arr_anchor, arr_offset)
    partial = jnp.dot(weights, arrived[:, :row_width], preferred_element_type=jnp.float32)
    if pow2:
        summed = halving_reduce(partial, time_groups)
    else:
        summed = lax.psum_scatter(partial, "tm", scatter_dimension=0, tiled=True)
    grid = summed.astype(jnp.bfloat16)
    grid_re, grid_im = grid[:, :NCH], grid[:, NCH:]
    lhs = jnp.concatenate(
        [grid, jnp.concatenate([grid_im, -grid_re], axis=1)], axis=0
    )
    out_scale = 4.0 / math.sqrt(NCH * time_groups * ROWS_DEV)
    both = jnp.dot(lhs[:, :NCH], tap_cos, preferred_element_type=jnp.float32) + jnp.dot(
        lhs[:, NCH:], tap_sin, preferred_element_type=jnp.float32
    )
    both = both * out_scale
    cells_out = grid.shape[0]
    return jnp.concatenate([both[:cells_out], both[cells_out:]], axis=1)


def solution(mesh):
    in_specs = (
        P("tm", "uv", None),
        P("tm", "uv"),
        P("tm", "uv"),
        P("tm", "uv", None, None),
        P("tm", "uv", None),
    )
    out_specs = P(("uv", "tm"), None)
    return jax.shard_map(
        per_device, mesh=mesh, in_specs=in_specs, out_specs=out_specs, check_vma=False
    )
```

```python
import math

import jax
import jax.numpy as jnp
from jax import lax
from jax.sharding import PartitionSpec as P

NCH = 1024
ROWS_DEV = 128
TS = 16
KTAPS = 8
OSAMP = 8
META = 128
SPLIT = 32


def kernel_taps(offsets):
    tap_index = jnp.arange(KTAPS, dtype=jnp.float32)
    sub_shift = (offsets.astype(jnp.float32) + 0.5) / OSAMP
    distance = tap_index[None, :] - (KTAPS / 2 - 1.0) - sub_shift[:, None]
    return jnp.exp(-distance * distance / (2.0 * 1.2 * 1.2))


def tap_matrix(cell_ids, anchors, offsets):
    span = TS - KTAPS + 1
    anchor_y = anchors // span
    anchor_x = anchors % span
    taps_y = kernel_taps(offsets // OSAMP)
    taps_x = kernel_taps(offsets % OSAMP)
    cell_y = cell_ids // TS
    cell_x = cell_ids % TS
    along_y = jnp.zeros((cell_ids.shape[0], anchors.shape[0]), jnp.float32)
    along_x = jnp.zeros((cell_ids.shape[0], anchors.shape[0]), jnp.float32)
    for step in range(KTAPS):
        along_y = along_y + jnp.where(
            cell_y[:, None] == anchor_y[None, :] + step, taps_y[None, :, step], 0.0
        )
        along_x = along_x + jnp.where(
            cell_x[:, None] == anchor_x[None, :] + step, taps_x[None, :, step], 0.0
        )
    return (along_y * along_x).astype(jnp.bfloat16)


def delay_halves():
    freq = jnp.arange(NCH, dtype=jnp.int32)
    hi = jnp.arange(NCH // SPLIT, dtype=jnp.int32)
    lo = jnp.arange(SPLIT, dtype=jnp.int32)
    scale = 2.0 * math.pi / NCH
    ang_hi = scale * ((freq[:, None] * (SPLIT * hi)[None, :]) % NCH).astype(jnp.float32)
    ang_lo = scale * ((freq[:, None] * lo[None, :]) % NCH).astype(jnp.float32)
    c_hi, s_hi = jnp.cos(ang_hi), jnp.sin(ang_hi)
    c_lo, s_lo = jnp.cos(ang_lo), jnp.sin(ang_lo)
    cosine = c_hi[:, :, None] * c_lo[:, None, :] - s_hi[:, :, None] * s_lo[:, None, :]
    sine = s_hi[:, :, None] * c_lo[:, None, :] + c_hi[:, :, None] * s_lo[:, None, :]
    window_arg = 2.0 * math.pi * freq.astype(jnp.float32) / (NCH - 1)
    taper = (
        0.35875
        - 0.48829 * jnp.cos(window_arg)
        + 0.14128 * jnp.cos(2.0 * window_arg)
        - 0.01168 * jnp.cos(3.0 * window_arg)
    )
    tap_cos = (taper[:, None, None] * cosine).reshape(NCH, NCH)
    tap_sin = (taper[:, None, None] * sine).reshape(NCH, NCH)
    return jnp.concatenate([tap_cos, tap_sin], axis=0).astype(jnp.bfloat16)


def halving_order(tm_index, time_groups, cell_share):
    level_bits = int(math.log2(time_groups))
    quarter = jnp.zeros((time_groups,), jnp.int32)
    for j in range(time_groups):
        value = tm_index
        pos = j
        for level in range(level_bits):
            half = time_groups >> (level + 1)
            sent = pos < half
            bit = 1 << level
            value = jnp.where(sent, value ^ bit, value)
            pos = pos % half if half > 0 else pos
        quarter = quarter.at[j].set(value)
    cells = quarter[:, None] * cell_share + jnp.arange(cell_share, dtype=jnp.int32)[None, :]
    return cells.reshape(-1)


def halving_reduce(partial, time_groups):
    level_bits = int(math.log2(time_groups))
    for level in range(level_bits):
        half = partial.shape[0] // 2
        bit = 1 << level
        perm = [(i, i ^ bit) for i in range(time_groups)]
        outgoing = partial[:half]
        if level > 0:
            outgoing = outgoing.astype(jnp.bfloat16)
        received = lax.ppermute(outgoing, "tm", perm)
        partial = partial[half:] + received.astype(jnp.float32)
    return partial


def uv_exchange(outgoing, uv_size):
    if uv_size > 16:
        return lax.all_to_all(outgoing, "uv", split_axis=0, concat_axis=0, tiled=True)
    uv_index = lax.axis_index("uv")
    pieces = [lax.dynamic_index_in_dim(outgoing, uv_index, 0, keepdims=False)]
    for shift in range(1, uv_size):
        perm = [(i, (i + shift) % uv_size) for i in range(uv_size)]
        piece = lax.dynamic_index_in_dim(outgoing, (uv_index + shift) % uv_size, 0, keepdims=False)
        pieces.append(lax.ppermute(piece, "uv", perm))
    return jnp.stack(pieces)


def per_device(visibility, anchor, offset, slot_rows, counts):
    time_groups = lax.axis_size("tm")
    uv_size = lax.axis_size("uv")
    cell_share = TS * TS // time_groups
    vis_rows = visibility[0]
    row_count, row_width = vis_rows.shape
    tile_count, slot_depth = slot_rows.shape[2:]
    slot_size = tile_count * slot_depth
    ints = jnp.concatenate(
        [slot_rows.reshape(-1), counts.reshape(-1), anchor.reshape(-1), offset.reshape(-1)]
    )
    flat_index = ints[:slot_size]
    live_count = ints[slot_size:slot_size + tile_count]
    anchor_row = ints[slot_size + tile_count:slot_size + tile_count + row_count]
    offset_row = ints[slot_size + tile_count + row_count:]
    is_live = (jnp.arange(slot_depth, dtype=jnp.int32)[None, :] < live_count[:, None]).reshape(-1)
    pick = (
        (flat_index[:, None] == jnp.arange(row_count, dtype=jnp.int32)[None, :]) & is_live[:, None]
    ).astype(jnp.bfloat16)
    picked = jnp.dot(pick, vis_rows, preferred_element_type=jnp.float32).astype(jnp.bfloat16)
    meta_rows = jnp.concatenate(
        [anchor_row[None, :], offset_row[None, :], jnp.zeros((META - 2, row_count), jnp.int32)],
        axis=0,
    ).astype(jnp.bfloat16)
    meta = lax.dot_general(
        pick, meta_rows, (((1,), (1,)), ((), ())), preferred_element_type=jnp.float32
    ).astype(jnp.bfloat16)
    outgoing = jnp.concatenate([picked, meta], axis=1).reshape(tile_count, slot_depth, row_width + META)
    arrived = uv_exchange(outgoing, uv_size)
    arrived = arrived.reshape(-1, row_width + META)
    arr_anchor = arrived[:, row_width].astype(jnp.int32)
    arr_offset = arrived[:, row_width + 1].astype(jnp.int32)
    tm_index = lax.axis_index("tm")
    pow2 = time_groups & (time_groups - 1) == 0
    if pow2:
        cells = halving_order(tm_index, time_groups, cell_share)
    else:
        cells = jnp.arange(TS * TS, dtype=jnp.int32)
    weights = tap_matrix(cells, arr_anchor, arr_offset)
    partial = jnp.dot(weights, arrived[:, :row_width], preferred_element_type=jnp.float32)
    if pow2:
        summed = halving_reduce(partial, time_groups)
    else:
        summed = lax.psum_scatter(partial, "tm", scatter_dimension=0, tiled=True)
    grid = summed.astype(jnp.bfloat16)
    grid_re, grid_im = grid[:, :NCH], grid[:, NCH:]
    lhs = jnp.concatenate(
        [grid, jnp.concatenate([grid_im, -grid_re], axis=1)], axis=0
    )
    out_scale = 4.0 / math.sqrt(NCH * time_groups * ROWS_DEV)
    both = jnp.dot(lhs, delay_halves(), preferred_element_type=jnp.float32) * out_scale
    cells_out = grid.shape[0]
    return jnp.concatenate([both[:cells_out], both[cells_out:]], axis=1)


def solution(mesh):
    in_specs = (
        P("tm", "uv", None),
        P("tm", "uv"),
        P("tm", "uv"),
        P("tm", "uv", None, None),
        P("tm", "uv", None),
    )
    out_specs = P(("uv", "tm"), None)
    return jax.shard_map(
        per_device, mesh=mesh, in_specs=in_specs, out_specs=out_specs, check_vma=False
    )
```

```python
import math

import jax
import jax.numpy as jnp
from jax import lax
from jax.sharding import PartitionSpec as P

NCH = 1024
ROWS_DEV = 128
TS = 16
KTAPS = 8
OSAMP = 8
META = 128
SPLIT = 32


def kernel_taps(offsets):
    tap_index = jnp.arange(KTAPS, dtype=jnp.float32)
    sub_shift = (offsets.astype(jnp.float32) + 0.5) / OSAMP
    distance = tap_index[None, :] - (KTAPS / 2 - 1.0) - sub_shift[:, None]
    return jnp.exp(-distance * distance / (2.0 * 1.2 * 1.2))


def tap_matrix(cell_ids, anchors, offsets):
    span = TS - KTAPS + 1
    anchor_y = anchors // span
    anchor_x = anchors % span
    taps_y = kernel_taps(offsets // OSAMP)
    taps_x = kernel_taps(offsets % OSAMP)
    cell_y = cell_ids // TS
    cell_x = cell_ids % TS
    along_y = jnp.zeros((cell_ids.shape[0], anchors.shape[0]), jnp.float32)
    along_x = jnp.zeros((cell_ids.shape[0], anchors.shape[0]), jnp.float32)
    for step in range(KTAPS):
        along_y = along_y + jnp.where(
            cell_y[:, None] == anchor_y[None, :] + step, taps_y[None, :, step], 0.0
        )
        along_x = along_x + jnp.where(
            cell_x[:, None] == anchor_x[None, :] + step, taps_x[None, :, step], 0.0
        )
    return (along_y * along_x).astype(jnp.bfloat16)


def delay_halves():
    freq = jnp.arange(NCH, dtype=jnp.int32)
    hi = jnp.arange(NCH // SPLIT, dtype=jnp.int32)
    lo = jnp.arange(SPLIT, dtype=jnp.int32)
    scale = 2.0 * math.pi / NCH
    ang_hi = scale * ((freq[:, None] * (SPLIT * hi)[None, :]) % NCH).astype(jnp.float32)
    ang_lo = scale * ((freq[:, None] * lo[None, :]) % NCH).astype(jnp.float32)
    c_hi, s_hi = jnp.cos(ang_hi), jnp.sin(ang_hi)
    c_lo, s_lo = jnp.cos(ang_lo), jnp.sin(ang_lo)
    cosine = c_hi[:, :, None] * c_lo[:, None, :] - s_hi[:, :, None] * s_lo[:, None, :]
    sine = s_hi[:, :, None] * c_lo[:, None, :] + c_hi[:, :, None] * s_lo[:, None, :]
    window_arg = 2.0 * math.pi * freq.astype(jnp.float32) / (NCH - 1)
    taper = (
        0.35875
        - 0.48829 * jnp.cos(window_arg)
        + 0.14128 * jnp.cos(2.0 * window_arg)
        - 0.01168 * jnp.cos(3.0 * window_arg)
    )
    tap_cos = (taper[:, None, None] * cosine).reshape(NCH, NCH)
    tap_sin = (taper[:, None, None] * sine).reshape(NCH, NCH)
    return jnp.concatenate([tap_cos, tap_sin], axis=0).astype(jnp.bfloat16)


def halving_order(tm_index, time_groups, cell_share):
    level_bits = int(math.log2(time_groups))
    quarter = jnp.zeros((time_groups,), jnp.int32)
    for j in range(time_groups):
        value = tm_index
        pos = j
        for level in range(level_bits):
            half = time_groups >> (level + 1)
            sent = pos < half
            bit = 1 << level
            value = jnp.where(sent, value ^ bit, value)
            pos = pos % half if half > 0 else pos
        quarter = quarter.at[j].set(value)
    cells = quarter[:, None] * cell_share + jnp.arange(cell_share, dtype=jnp.int32)[None, :]
    return cells.reshape(-1)


def halving_reduce(partial, time_groups):
    level_bits = int(math.log2(time_groups))
    for level in range(level_bits):
        half = partial.shape[0] // 2
        bit = 1 << level
        perm = [(i, i ^ bit) for i in range(time_groups)]
        outgoing = partial[:half]
        if level > 0:
            outgoing = outgoing.astype(jnp.bfloat16)
        received = lax.ppermute(outgoing, "tm", perm)
        partial = partial[half:] + received.astype(jnp.float32)
    return partial


def uv_exchange(outgoing, uv_size):
    if uv_size > 16:
        return lax.all_to_all(outgoing, "uv", split_axis=0, concat_axis=0, tiled=True)
    pieces = [outgoing[0]]
    for shift in range(1, uv_size):
        perm = [(i, (i + shift) % uv_size) for i in range(uv_size)]
        pieces.append(lax.ppermute(outgoing[shift], "uv", perm))
    return jnp.stack(pieces)


def per_device(visibility, anchor, offset, slot_rows, counts):
    time_groups = lax.axis_size("tm")
    uv_size = lax.axis_size("uv")
    cell_share = TS * TS // time_groups
    vis_rows = visibility[0]
    row_count, row_width = vis_rows.shape
    tile_count, slot_depth = slot_rows.shape[2:]
    slot_size = tile_count * slot_depth
    (ints,) = lax.optimization_barrier(
        (
            jnp.concatenate(
                [slot_rows.reshape(-1), counts.reshape(-1), anchor.reshape(-1), offset.reshape(-1)]
            ),
        )
    )
    slot_table = ints[:slot_size].reshape(tile_count, slot_depth)
    live_count = ints[slot_size:slot_size + tile_count]
    anchor_row = ints[slot_size + tile_count:slot_size + tile_count + row_count]
    offset_row = ints[slot_size + tile_count + row_count:]
    if uv_size <= 16:
        uv_index = lax.axis_index("uv")
        slot_table = lax.dynamic_slice_in_dim(
            jnp.concatenate([slot_table, slot_table], axis=0), uv_index, tile_count, 0
        )
        live_count = lax.dynamic_slice_in_dim(
            jnp.concatenate([live_count, live_count], axis=0), uv_index, tile_count, 0
        )
    is_live = (jnp.arange(slot_depth, dtype=jnp.int32)[None, :] < live_count[:, None]).reshape(-1)
    flat_index = slot_table.reshape(-1)
    pick = (
        (flat_index[:, None] == jnp.arange(row_count, dtype=jnp.int32)[None, :]) & is_live[:, None]
    ).astype(jnp.bfloat16)
    picked = jnp.dot(pick, vis_rows, preferred_element_type=jnp.float32).astype(jnp.bfloat16)
    meta_rows = jnp.concatenate(
        [anchor_row[None, :], offset_row[None, :], jnp.zeros((META - 2, row_count), jnp.int32)],
        axis=0,
    ).astype(jnp.bfloat16)
    meta = lax.dot_general(
        pick, meta_rows, (((1,), (1,)), ((), ())), preferred_element_type=jnp.float32
    ).astype(jnp.bfloat16)
    outgoing = jnp.concatenate([picked, meta], axis=1).reshape(tile_count, slot_depth, row_width + META)
    arrived = uv_exchange(outgoing, uv_size)
    arrived = arrived.reshape(-1, row_width + META)
    arr_anchor = arrived[:, row_width].astype(jnp.int32)
    arr_offset = arrived[:, row_width + 1].astype(jnp.int32)
    tm_index = lax.axis_index("tm")
    pow2 = time_groups & (time_groups - 1) == 0
    if pow2:
        cells = halving_order(tm_index, time_groups, cell_share)
    else:
        cells = jnp.arange(TS * TS, dtype=jnp.int32)
    weights = tap_matrix(cells, arr_anchor, arr_offset)
    partial = jnp.dot(weights, arrived[:, :row_width], preferred_element_type=jnp.float32)
    if pow2:
        summed = halving_reduce(partial, time_groups)
    else:
        summed = lax.psum_scatter(partial, "tm", scatter_dimension=0, tiled=True)
    grid = summed.astype(jnp.bfloat16)
    grid_re, grid_im = grid[:, :NCH], grid[:, NCH:]
    lhs = jnp.concatenate(
        [grid, jnp.concatenate([grid_im, -grid_re], axis=1)], axis=0
    )
    out_scale = 4.0 / math.sqrt(NCH * time_groups * ROWS_DEV)
    both = jnp.dot(lhs, delay_halves(), preferred_element_type=jnp.float32) * out_scale
    cells_out = grid.shape[0]
    return jnp.concatenate([both[:cells_out], both[cells_out:]], axis=1)


def solution(mesh):
    in_specs = (
        P("tm", "uv", None),
        P("tm", "uv"),
        P("tm", "uv"),
        P("tm", "uv", None, None),
        P("tm", "uv", None),
    )
    out_specs = P(("uv", "tm"), None)
    return jax.shard_map(
        per_device, mesh=mesh, in_specs=in_specs, out_specs=out_specs, check_vma=False
    )
```

```python
import math

import jax
import jax.numpy as jnp
from jax import lax
from jax.sharding import PartitionSpec as P

NCH = 1024
ROWS_DEV = 128
TS = 16
KTAPS = 8
OSAMP = 8
META = 128
SPLIT = 32


def kernel_taps(offsets):
    tap_index = jnp.arange(KTAPS, dtype=jnp.float32)
    sub_shift = (offsets.astype(jnp.float32) + 0.5) / OSAMP
    distance = tap_index[None, :] - (KTAPS / 2 - 1.0) - sub_shift[:, None]
    return jnp.exp(-distance * distance / (2.0 * 1.2 * 1.2))


def tap_matrix(cell_ids, anchors, offsets):
    span = TS - KTAPS + 1
    anchor_y = anchors // span
    anchor_x = anchors % span
    taps_y = kernel_taps(offsets // OSAMP)
    taps_x = kernel_taps(offsets % OSAMP)
    cell_y = cell_ids // TS
    cell_x = cell_ids % TS
    along_y = jnp.zeros((cell_ids.shape[0], anchors.shape[0]), jnp.float32)
    along_x = jnp.zeros((cell_ids.shape[0], anchors.shape[0]), jnp.float32)
    for step in range(KTAPS):
        along_y = along_y + jnp.where(
            cell_y[:, None] == anchor_y[None, :] + step, taps_y[None, :, step], 0.0
        )
        along_x = along_x + jnp.where(
            cell_x[:, None] == anchor_x[None, :] + step, taps_x[None, :, step], 0.0
        )
    return (along_y * along_x).astype(jnp.bfloat16)


def delay_halves(freq):
    hi = jnp.arange(NCH // SPLIT, dtype=jnp.int32)
    lo = jnp.arange(SPLIT, dtype=jnp.int32)
    scale = 2.0 * math.pi / NCH
    ang_hi = scale * ((freq[:, None] * (SPLIT * hi)[None, :]) % NCH).astype(jnp.float32)
    ang_lo = scale * ((freq[:, None] * lo[None, :]) % NCH).astype(jnp.float32)
    c_hi, s_hi = jnp.cos(ang_hi), jnp.sin(ang_hi)
    c_lo, s_lo = jnp.cos(ang_lo), jnp.sin(ang_lo)
    cosine = c_hi[:, :, None] * c_lo[:, None, :] - s_hi[:, :, None] * s_lo[:, None, :]
    sine = s_hi[:, :, None] * c_lo[:, None, :] + c_hi[:, :, None] * s_lo[:, None, :]
    window_arg = 2.0 * math.pi * freq.astype(jnp.float32) / (NCH - 1)
    taper = (
        0.35875
        - 0.48829 * jnp.cos(window_arg)
        + 0.14128 * jnp.cos(2.0 * window_arg)
        - 0.01168 * jnp.cos(3.0 * window_arg)
    )
    tap_cos = (taper[:, None, None] * cosine).reshape(NCH, NCH)
    tap_sin = (taper[:, None, None] * sine).reshape(NCH, NCH)
    return jnp.concatenate([tap_cos, tap_sin], axis=0).astype(jnp.bfloat16)


def halving_order(tm_index, time_groups, cell_share):
    level_bits = int(math.log2(time_groups))
    quarter = jnp.zeros((time_groups,), jnp.int32)
    for j in range(time_groups):
        value = tm_index
        pos = j
        for level in range(level_bits):
            half = time_groups >> (level + 1)
            sent = pos < half
            bit = 1 << level
            value = jnp.where(sent, value ^ bit, value)
            pos = pos % half if half > 0 else pos
        quarter = quarter.at[j].set(value)
    cells = quarter[:, None] * cell_share + jnp.arange(cell_share, dtype=jnp.int32)[None, :]
    return cells.reshape(-1)


def halving_reduce(partial, time_groups, gated=None):
    level_bits = int(math.log2(time_groups))
    for level in range(level_bits):
        if level == 1 and gated is not None:
            partial, gated = lax.optimization_barrier((partial, gated))
        half = partial.shape[0] // 2
        bit = 1 << level
        perm = [(i, i ^ bit) for i in range(time_groups)]
        outgoing = partial[:half]
        if level > 0:
            outgoing = outgoing.astype(jnp.bfloat16)
        received = lax.ppermute(outgoing, "tm", perm)
        partial = partial[half:] + received.astype(jnp.float32)
    return partial, gated


def uv_exchange(outgoing, uv_size):
    if uv_size > 16:
        return lax.all_to_all(outgoing, "uv", split_axis=0, concat_axis=0, tiled=True)
    pieces = [outgoing[0]]
    for shift in range(1, uv_size):
        perm = [(i, (i + shift) % uv_size) for i in range(uv_size)]
        pieces.append(lax.ppermute(outgoing[shift], "uv", perm))
    return jnp.stack(pieces)


def per_device(visibility, anchor, offset, slot_rows, counts):
    time_groups = lax.axis_size("tm")
    uv_size = lax.axis_size("uv")
    cell_share = TS * TS // time_groups
    vis_rows = visibility[0]
    row_count, row_width = vis_rows.shape
    tile_count, slot_depth = slot_rows.shape[2:]
    slot_size = tile_count * slot_depth
    (ints,) = lax.optimization_barrier(
        (
            jnp.concatenate(
                [slot_rows.reshape(-1), counts.reshape(-1), anchor.reshape(-1), offset.reshape(-1)]
            ),
        )
    )
    slot_table = ints[:slot_size].reshape(tile_count, slot_depth)
    live_count = ints[slot_size:slot_size + tile_count]
    anchor_row = ints[slot_size + tile_count:slot_size + tile_count + row_count]
    offset_row = ints[slot_size + tile_count + row_count:]
    if uv_size <= 16:
        uv_index = lax.axis_index("uv")
        slot_table = lax.dynamic_slice_in_dim(
            jnp.concatenate([slot_table, slot_table], axis=0), uv_index, tile_count, 0
        )
        live_count = lax.dynamic_slice_in_dim(
            jnp.concatenate([live_count, live_count], axis=0), uv_index, tile_count, 0
        )
    is_live = (jnp.arange(slot_depth, dtype=jnp.int32)[None, :] < live_count[:, None]).reshape(-1)
    flat_index = slot_table.reshape(-1)
    pick = (
        (flat_index[:, None] == jnp.arange(row_count, dtype=jnp.int32)[None, :]) & is_live[:, None]
    ).astype(jnp.bfloat16)
    picked = jnp.dot(pick, vis_rows, preferred_element_type=jnp.float32).astype(jnp.bfloat16)
    meta_rows = jnp.concatenate(
        [anchor_row[None, :], offset_row[None, :], jnp.zeros((META - 2, row_count), jnp.int32)],
        axis=0,
    ).astype(jnp.bfloat16)
    meta = lax.dot_general(
        pick, meta_rows, (((1,), (1,)), ((), ())), preferred_element_type=jnp.float32
    ).astype(jnp.bfloat16)
    outgoing = jnp.concatenate([picked, meta], axis=1).reshape(tile_count, slot_depth, row_width + META)
    arrived = uv_exchange(outgoing, uv_size)
    arrived = arrived.reshape(-1, row_width + META)
    arr_anchor = arrived[:, row_width].astype(jnp.int32)
    arr_offset = arrived[:, row_width + 1].astype(jnp.int32)
    tm_index = lax.axis_index("tm")
    pow2 = time_groups & (time_groups - 1) == 0
    if pow2:
        cells = halving_order(tm_index, time_groups, cell_share)
    else:
        cells = jnp.arange(TS * TS, dtype=jnp.int32)
    weights = tap_matrix(cells, arr_anchor, arr_offset)
    partial = jnp.dot(weights, arrived[:, :row_width], preferred_element_type=jnp.float32)
    freq = jnp.arange(NCH, dtype=jnp.int32)
    if pow2 and time_groups > 2:
        summed, freq = halving_reduce(partial, time_groups, freq)
    elif pow2:
        summed, _ = halving_reduce(partial, time_groups)
    else:
        summed = lax.psum_scatter(partial, "tm", scatter_dimension=0, tiled=True)
    grid = summed.astype(jnp.bfloat16)
    grid_re, grid_im = grid[:, :NCH], grid[:, NCH:]
    lhs = jnp.concatenate(
        [grid, jnp.concatenate([grid_im, -grid_re], axis=1)], axis=0
    )
    out_scale = 4.0 / math.sqrt(NCH * time_groups * ROWS_DEV)
    both = jnp.dot(lhs, delay_halves(freq), preferred_element_type=jnp.float32) * out_scale
    cells_out = grid.shape[0]
    return jnp.concatenate([both[:cells_out], both[cells_out:]], axis=1)


def solution(mesh):
    in_specs = (
        P("tm", "uv", None),
        P("tm", "uv"),
        P("tm", "uv"),
        P("tm", "uv", None, None),
        P("tm", "uv", None),
    )
    out_specs = P(("uv", "tm"), None)
    return jax.shard_map(
        per_device, mesh=mesh, in_specs=in_specs, out_specs=out_specs, check_vma=False
    )
```

```python
import math

import jax
import jax.numpy as jnp
from jax import lax
from jax.sharding import PartitionSpec as P

NCH = 1024
ROWS_DEV = 128
TS = 16
KTAPS = 8
OSAMP = 8
META = 128
SPLIT = 32


def kernel_taps(offsets):
    tap_index = jnp.arange(KTAPS, dtype=jnp.float32)
    sub_shift = (offsets.astype(jnp.float32) + 0.5) / OSAMP
    distance = tap_index[None, :] - (KTAPS / 2 - 1.0) - sub_shift[:, None]
    return jnp.exp(-distance * distance / (2.0 * 1.2 * 1.2))


def tap_matrix(cell_ids, anchors, offsets):
    span = TS - KTAPS + 1
    anchor_y = anchors // span
    anchor_x = anchors % span
    taps_y = kernel_taps(offsets // OSAMP)
    taps_x = kernel_taps(offsets % OSAMP)
    cell_y = cell_ids // TS
    cell_x = cell_ids % TS
    along_y = jnp.zeros((cell_ids.shape[0], anchors.shape[0]), jnp.float32)
    along_x = jnp.zeros((cell_ids.shape[0], anchors.shape[0]), jnp.float32)
    for step in range(KTAPS):
        along_y = along_y + jnp.where(
            cell_y[:, None] == anchor_y[None, :] + step, taps_y[None, :, step], 0.0
        )
        along_x = along_x + jnp.where(
            cell_x[:, None] == anchor_x[None, :] + step, taps_x[None, :, step], 0.0
        )
    return (along_y * along_x).astype(jnp.bfloat16)


def delay_halves():
    freq = jnp.arange(NCH, dtype=jnp.int32)
    hi = jnp.arange(NCH // SPLIT, dtype=jnp.int32)
    lo = jnp.arange(SPLIT, dtype=jnp.int32)
    scale = 2.0 * math.pi / NCH
    ang_hi = scale * ((freq[:, None] * (SPLIT * hi)[None, :]) % NCH).astype(jnp.float32)
    ang_lo = scale * ((freq[:, None] * lo[None, :]) % NCH).astype(jnp.float32)
    c_hi, s_hi = jnp.cos(ang_hi), jnp.sin(ang_hi)
    c_lo, s_lo = jnp.cos(ang_lo), jnp.sin(ang_lo)
    cosine = c_hi[:, :, None] * c_lo[:, None, :] - s_hi[:, :, None] * s_lo[:, None, :]
    sine = s_hi[:, :, None] * c_lo[:, None, :] + c_hi[:, :, None] * s_lo[:, None, :]
    window_arg = 2.0 * math.pi * freq.astype(jnp.float32) / (NCH - 1)
    taper = (
        0.35875
        - 0.48829 * jnp.cos(window_arg)
        + 0.14128 * jnp.cos(2.0 * window_arg)
        - 0.01168 * jnp.cos(3.0 * window_arg)
    )
    tap_cos = (taper[:, None, None] * cosine).reshape(NCH, NCH)
    tap_sin = (taper[:, None, None] * sine).reshape(NCH, NCH)
    return jnp.concatenate([tap_cos, tap_sin], axis=0).astype(jnp.bfloat16)


def halving_order(tm_index, time_groups, cell_share):
    level_bits = int(math.log2(time_groups))
    quarter = jnp.zeros((time_groups,), jnp.int32)
    for j in range(time_groups):
        value = tm_index
        pos = j
        for level in range(level_bits):
            half = time_groups >> (level + 1)
            sent = pos < half
            bit = 1 << level
            value = jnp.where(sent, value ^ bit, value)
            pos = pos % half if half > 0 else pos
        quarter = quarter.at[j].set(value)
    cells = quarter[:, None] * cell_share + jnp.arange(cell_share, dtype=jnp.int32)[None, :]
    return cells.reshape(-1)


def halving_reduce(partial, time_groups):
    level_bits = int(math.log2(time_groups))
    for level in range(level_bits):
        half = partial.shape[0] // 2
        bit = 1 << level
        perm = [(i, i ^ bit) for i in range(time_groups)]
        outgoing = partial[:half]
        if level > 0:
            outgoing = outgoing.astype(jnp.bfloat16)
        received = lax.ppermute(outgoing, "tm", perm)
        partial = partial[half:] + received.astype(jnp.float32)
    return partial


def uv_exchange(outgoing, uv_size):
    if uv_size > 16:
        return lax.all_to_all(outgoing, "uv", split_axis=0, concat_axis=0, tiled=True)
    pieces = [outgoing[0]]
    for shift in range(1, uv_size):
        perm = [(i, (i + shift) % uv_size) for i in range(uv_size)]
        pieces.append(lax.ppermute(outgoing[shift], "uv", perm))
    return jnp.stack(pieces)


def per_device(visibility, anchor, offset, slot_rows, counts):
    time_groups = lax.axis_size("tm")
    uv_size = lax.axis_size("uv")
    cell_share = TS * TS // time_groups
    vis_rows = visibility[0]
    row_count, row_width = vis_rows.shape
    tile_count, slot_depth = slot_rows.shape[2:]
    slot_size = tile_count * slot_depth
    lanes = max(row_count, slot_depth, tile_count)
    pad = lambda x: jnp.pad(x, ((0, 0), (0, lanes - x.shape[1])))
    (ints,) = lax.optimization_barrier(
        (
            jnp.concatenate(
                [pad(slot_rows[0, 0]), pad(counts[0]), pad(anchor), pad(offset)], axis=0
            ),
        )
    )
    slot_table = ints[:tile_count, :slot_depth]
    live_count = ints[tile_count, :tile_count]
    anchor_row = ints[tile_count + 1, :row_count]
    offset_row = ints[tile_count + 2, :row_count]
    if uv_size <= 16:
        uv_index = lax.axis_index("uv")
        slot_table = lax.dynamic_slice_in_dim(
            jnp.concatenate([slot_table, slot_table], axis=0), uv_index, tile_count, 0
        )
        live_count = lax.dynamic_slice_in_dim(
            jnp.concatenate([live_count, live_count], axis=0), uv_index, tile_count, 0
        )
    is_live = (jnp.arange(slot_depth, dtype=jnp.int32)[None, :] < live_count[:, None]).reshape(-1)
    flat_index = slot_table.reshape(-1)
    pick = (
        (flat_index[:, None] == jnp.arange(row_count, dtype=jnp.int32)[None, :]) & is_live[:, None]
    ).astype(jnp.bfloat16)
    picked = jnp.dot(pick, vis_rows, preferred_element_type=jnp.float32).astype(jnp.bfloat16)
    meta_rows = jnp.concatenate(
        [anchor_row[None, :], offset_row[None, :], jnp.zeros((META - 2, row_count), jnp.int32)],
        axis=0,
    ).astype(jnp.bfloat16)
    meta = lax.dot_general(
        pick, meta_rows, (((1,), (1,)), ((), ())), preferred_element_type=jnp.float32
    ).astype(jnp.bfloat16)
    outgoing = jnp.concatenate([picked, meta], axis=1).reshape(tile_count, slot_depth, row_width + META)
    arrived = uv_exchange(outgoing, uv_size)
    arrived = arrived.reshape(-1, row_width + META)
    arr_anchor = arrived[:, row_width].astype(jnp.int32)
    arr_offset = arrived[:, row_width + 1].astype(jnp.int32)
    tm_index = lax.axis_index("tm")
    pow2 = time_groups & (time_groups - 1) == 0
    if pow2:
        cells = halving_order(tm_index, time_groups, cell_share)
    else:
        cells = jnp.arange(TS * TS, dtype=jnp.int32)
    weights = tap_matrix(cells, arr_anchor, arr_offset)
    partial = jnp.dot(weights, arrived[:, :row_width], preferred_element_type=jnp.float32)
    if pow2:
        summed = halving_reduce(partial, time_groups)
    else:
        summed = lax.psum_scatter(partial, "tm", scatter_dimension=0, tiled=True)
    grid = summed.astype(jnp.bfloat16)
    grid_re, grid_im = grid[:, :NCH], grid[:, NCH:]
    lhs = jnp.concatenate(
        [grid, jnp.concatenate([grid_im, -grid_re], axis=1)], axis=0
    )
    out_scale = 4.0 / math.sqrt(NCH * time_groups * ROWS_DEV)
    both = jnp.dot(lhs, delay_halves(), preferred_element_type=jnp.float32) * out_scale
    cells_out = grid.shape[0]
    return jnp.concatenate([both[:cells_out], both[cells_out:]], axis=1)


def solution(mesh):
    in_specs = (
        P("tm", "uv", None),
        P("tm", "uv"),
        P("tm", "uv"),
        P("tm", "uv", None, None),
        P("tm", "uv", None),
    )
    out_specs = P(("uv", "tm"), None)
    return jax.shard_map(
        per_device, mesh=mesh, in_specs=in_specs, out_specs=out_specs, check_vma=False
    )
```

```python
import math

import jax
import jax.numpy as jnp
from jax import lax
from jax.sharding import PartitionSpec as P

NCH = 1024
ROWS_DEV = 128
TS = 16
KTAPS = 8
OSAMP = 8
META = 128
SPLIT = 32


def kernel_taps(offsets):
    tap_index = jnp.arange(KTAPS, dtype=jnp.float32)
    sub_shift = (offsets.astype(jnp.float32) + 0.5) / OSAMP
    distance = tap_index[None, :] - (KTAPS / 2 - 1.0) - sub_shift[:, None]
    return jnp.exp(-distance * distance / (2.0 * 1.2 * 1.2))


def tap_matrix(cell_ids, anchors, offsets):
    span = TS - KTAPS + 1
    anchor_y = anchors // span
    anchor_x = anchors % span
    taps_y = kernel_taps(offsets // OSAMP)
    taps_x = kernel_taps(offsets % OSAMP)
    cell_y = cell_ids // TS
    cell_x = cell_ids % TS
    along_y = jnp.zeros((cell_ids.shape[0], anchors.shape[0]), jnp.float32)
    along_x = jnp.zeros((cell_ids.shape[0], anchors.shape[0]), jnp.float32)
    for step in range(KTAPS):
        along_y = along_y + jnp.where(
            cell_y[:, None] == anchor_y[None, :] + step, taps_y[None, :, step], 0.0
        )
        along_x = along_x + jnp.where(
            cell_x[:, None] == anchor_x[None, :] + step, taps_x[None, :, step], 0.0
        )
    return (along_y * along_x).astype(jnp.bfloat16)


def delay_halves():
    freq = jnp.arange(NCH, dtype=jnp.int32)
    hi = jnp.arange(NCH // SPLIT, dtype=jnp.int32)
    lo = jnp.arange(SPLIT, dtype=jnp.int32)
    scale = 2.0 * math.pi / NCH
    ang_hi = scale * ((freq[:, None] * (SPLIT * hi)[None, :]) % NCH).astype(jnp.float32)
    ang_lo = scale * ((freq[:, None] * lo[None, :]) % NCH).astype(jnp.float32)
    c_hi, s_hi = jnp.cos(ang_hi), jnp.sin(ang_hi)
    c_lo, s_lo = jnp.cos(ang_lo), jnp.sin(ang_lo)
    cosine = c_hi[:, :, None] * c_lo[:, None, :] - s_hi[:, :, None] * s_lo[:, None, :]
    sine = s_hi[:, :, None] * c_lo[:, None, :] + c_hi[:, :, None] * s_lo[:, None, :]
    window_arg = 2.0 * math.pi * freq.astype(jnp.float32) / (NCH - 1)
    taper = (
        0.35875
        - 0.48829 * jnp.cos(window_arg)
        + 0.14128 * jnp.cos(2.0 * window_arg)
        - 0.01168 * jnp.cos(3.0 * window_arg)
    )
    tap_cos = (taper[:, None, None] * cosine).reshape(NCH, NCH)
    tap_sin = (taper[:, None, None] * sine).reshape(NCH, NCH)
    return jnp.concatenate([tap_cos, tap_sin], axis=0).astype(jnp.bfloat16)


def halving_order(tm_index, time_groups, cell_share):
    level_bits = int(math.log2(time_groups))
    quarter = jnp.zeros((time_groups,), jnp.int32)
    for j in range(time_groups):
        value = tm_index
        pos = j
        for level in range(level_bits):
            half = time_groups >> (level + 1)
            sent = pos < half
            bit = 1 << level
            value = jnp.where(sent, value ^ bit, value)
            pos = pos % half if half > 0 else pos
        quarter = quarter.at[j].set(value)
    cells = quarter[:, None] * cell_share + jnp.arange(cell_share, dtype=jnp.int32)[None, :]
    return cells.reshape(-1)


def halving_reduce(partial, time_groups):
    level_bits = int(math.log2(time_groups))
    for level in range(level_bits):
        half = partial.shape[0] // 2
        bit = 1 << level
        perm = [(i, i ^ bit) for i in range(time_groups)]
        outgoing = partial[:half]
        if level > 0:
            outgoing = outgoing.astype(jnp.bfloat16)
        received = lax.ppermute(outgoing, "tm", perm)
        partial = partial[half:] + received.astype(jnp.float32)
    return partial


def uv_exchange(outgoing, uv_size):
    if uv_size > 16 or uv_size & (uv_size - 1):
        return lax.all_to_all(outgoing, "uv", split_axis=0, concat_axis=0, tiled=True)
    pieces = [outgoing[0]]
    for mask in range(1, uv_size):
        perm = [(i, i ^ mask) for i in range(uv_size)]
        pieces.append(lax.ppermute(outgoing[mask], "uv", perm))
    return jnp.stack(pieces)


def xor_rows(table, index):
    rows = table.shape[0]
    bit = 1
    while bit < rows:
        split = table.reshape((rows // (2 * bit), 2, bit) + table.shape[1:])
        flipped = split[:, ::-1]
        table = jnp.where((index & bit) > 0, flipped, split).reshape(table.shape)
        bit *= 2
    return table


def per_device(visibility, anchor, offset, slot_rows, counts):
    time_groups = lax.axis_size("tm")
    uv_size = lax.axis_size("uv")
    cell_share = TS * TS // time_groups
    vis_rows = visibility[0]
    row_count, row_width = vis_rows.shape
    tile_count, slot_depth = slot_rows.shape[2:]
    slot_size = tile_count * slot_depth
    lanes = max(row_count, slot_depth, tile_count)
    pad = lambda x: jnp.pad(x, ((0, 0), (0, lanes - x.shape[1])))
    (ints,) = lax.optimization_barrier(
        (
            jnp.concatenate(
                [pad(slot_rows[0, 0]), pad(counts[0]), pad(anchor), pad(offset)], axis=0
            ),
        )
    )
    slot_table = ints[:tile_count, :slot_depth]
    live_count = ints[tile_count, :tile_count]
    anchor_row = ints[tile_count + 1, :row_count]
    offset_row = ints[tile_count + 2, :row_count]
    if uv_size <= 16 and uv_size & (uv_size - 1) == 0:
        uv_index = lax.axis_index("uv")
        slot_table = xor_rows(slot_table, uv_index)
        live_count = xor_rows(live_count, uv_index)
    is_live = (jnp.arange(slot_depth, dtype=jnp.int32)[None, :] < live_count[:, None]).reshape(-1)
    flat_index = slot_table.reshape(-1)
    pick = (
        (flat_index[:, None] == jnp.arange(row_count, dtype=jnp.int32)[None, :]) & is_live[:, None]
    ).astype(jnp.bfloat16)
    picked = jnp.dot(pick, vis_rows, preferred_element_type=jnp.float32).astype(jnp.bfloat16)
    meta_rows = jnp.concatenate(
        [anchor_row[None, :], offset_row[None, :], jnp.zeros((META - 2, row_count), jnp.int32)],
        axis=0,
    ).astype(jnp.bfloat16)
    meta = lax.dot_general(
        pick, meta_rows, (((1,), (1,)), ((), ())), preferred_element_type=jnp.float32
    ).astype(jnp.bfloat16)
    outgoing = jnp.concatenate([picked, meta], axis=1).reshape(tile_count, slot_depth, row_width + META)
    arrived = uv_exchange(outgoing, uv_size)
    arrived = arrived.reshape(-1, row_width + META)
    arr_anchor = arrived[:, row_width].astype(jnp.int32)
    arr_offset = arrived[:, row_width + 1].astype(jnp.int32)
    tm_index = lax.axis_index("tm")
    pow2 = time_groups & (time_groups - 1) == 0
    if pow2:
        cells = halving_order(tm_index, time_groups, cell_share)
    else:
        cells = jnp.arange(TS * TS, dtype=jnp.int32)
    weights = tap_matrix(cells, arr_anchor, arr_offset)
    partial = jnp.dot(weights, arrived[:, :row_width], preferred_element_type=jnp.float32)
    if pow2:
        summed = halving_reduce(partial, time_groups)
    else:
        summed = lax.psum_scatter(partial, "tm", scatter_dimension=0, tiled=True)
    grid = summed.astype(jnp.bfloat16)
    grid_re, grid_im = grid[:, :NCH], grid[:, NCH:]
    lhs = jnp.concatenate(
        [grid, jnp.concatenate([grid_im, -grid_re], axis=1)], axis=0
    )
    out_scale = 4.0 / math.sqrt(NCH * time_groups * ROWS_DEV)
    both = jnp.dot(lhs, delay_halves(), preferred_element_type=jnp.float32) * out_scale
    cells_out = grid.shape[0]
    return jnp.concatenate([both[:cells_out], both[cells_out:]], axis=1)


def solution(mesh):
    in_specs = (
        P("tm", "uv", None),
        P("tm", "uv"),
        P("tm", "uv"),
        P("tm", "uv", None, None),
        P("tm", "uv", None),
    )
    out_specs = P(("uv", "tm"), None)
    return jax.shard_map(
        per_device, mesh=mesh, in_specs=in_specs, out_specs=out_specs, check_vma=False
    )
```

```python
import math

import jax
import jax.numpy as jnp
from jax import lax
from jax.sharding import PartitionSpec as P

NCH = 1024
ROWS_DEV = 128
TS = 16
KTAPS = 8
OSAMP = 8
META = 128
SPLIT = 32


def kernel_taps(offsets):
    tap_index = jnp.arange(KTAPS, dtype=jnp.float32)
    sub_shift = (offsets.astype(jnp.float32) + 0.5) / OSAMP
    distance = tap_index[None, :] - (KTAPS / 2 - 1.0) - sub_shift[:, None]
    return jnp.exp(-distance * distance / (2.0 * 1.2 * 1.2))


def tap_matrix(cell_ids, anchors, offsets):
    span = TS - KTAPS + 1
    anchor_y = anchors // span
    anchor_x = anchors % span
    taps_y = kernel_taps(offsets // OSAMP)
    taps_x = kernel_taps(offsets % OSAMP)
    cell_y = cell_ids // TS
    cell_x = cell_ids % TS
    along_y = jnp.zeros((cell_ids.shape[0], anchors.shape[0]), jnp.float32)
    along_x = jnp.zeros((cell_ids.shape[0], anchors.shape[0]), jnp.float32)
    for step in range(KTAPS):
        along_y = along_y + jnp.where(
            cell_y[:, None] == anchor_y[None, :] + step, taps_y[None, :, step], 0.0
        )
        along_x = along_x + jnp.where(
            cell_x[:, None] == anchor_x[None, :] + step, taps_x[None, :, step], 0.0
        )
    return (along_y * along_x).astype(jnp.bfloat16)


def delay_halves():
    freq = jnp.arange(NCH, dtype=jnp.int32)
    hi = jnp.arange(NCH // SPLIT, dtype=jnp.int32)
    lo = jnp.arange(SPLIT, dtype=jnp.int32)
    scale = 2.0 * math.pi / NCH
    ang_hi = scale * ((freq[:, None] * (SPLIT * hi)[None, :]) % NCH).astype(jnp.float32)
    ang_lo = scale * ((freq[:, None] * lo[None, :]) % NCH).astype(jnp.float32)
    c_hi, s_hi = jnp.cos(ang_hi), jnp.sin(ang_hi)
    c_lo, s_lo = jnp.cos(ang_lo), jnp.sin(ang_lo)
    cosine = c_hi[:, :, None] * c_lo[:, None, :] - s_hi[:, :, None] * s_lo[:, None, :]
    sine = s_hi[:, :, None] * c_lo[:, None, :] + c_hi[:, :, None] * s_lo[:, None, :]
    window_arg = 2.0 * math.pi * freq.astype(jnp.float32) / (NCH - 1)
    taper = (
        0.35875
        - 0.48829 * jnp.cos(window_arg)
        + 0.14128 * jnp.cos(2.0 * window_arg)
        - 0.01168 * jnp.cos(3.0 * window_arg)
    )
    tap_cos = (taper[:, None, None] * cosine).reshape(NCH, NCH)
    tap_sin = (taper[:, None, None] * sine).reshape(NCH, NCH)
    upper = jnp.concatenate([tap_cos, -tap_sin], axis=1)
    lower = jnp.concatenate([tap_sin, tap_cos], axis=1)
    return jnp.concatenate([upper, lower], axis=0).astype(jnp.bfloat16)


def halving_order(tm_index, time_groups, cell_share):
    level_bits = int(math.log2(time_groups))
    quarter = jnp.zeros((time_groups,), jnp.int32)
    for j in range(time_groups):
        value = tm_index
        pos = j
        for level in range(level_bits):
            half = time_groups >> (level + 1)
            sent = pos < half
            bit = 1 << level
            value = jnp.where(sent, value ^ bit, value)
            pos = pos % half if half > 0 else pos
        quarter = quarter.at[j].set(value)
    cells = quarter[:, None] * cell_share + jnp.arange(cell_share, dtype=jnp.int32)[None, :]
    return cells.reshape(-1)


def halving_reduce(partial, time_groups):
    level_bits = int(math.log2(time_groups))
    for level in range(level_bits):
        half = partial.shape[0] // 2
        bit = 1 << level
        perm = [(i, i ^ bit) for i in range(time_groups)]
        outgoing = partial[:half]
        if level > 0:
            outgoing = outgoing.astype(jnp.bfloat16)
        received = lax.ppermute(outgoing, "tm", perm)
        partial = partial[half:] + received.astype(jnp.float32)
    return partial


def uv_exchange(outgoing, uv_size):
    if uv_size > 16:
        return lax.all_to_all(outgoing, "uv", split_axis=0, concat_axis=0, tiled=True)
    pieces = [outgoing[0]]
    for shift in range(1, uv_size):
        perm = [(i, (i + shift) % uv_size) for i in range(uv_size)]
        pieces.append(lax.ppermute(outgoing[shift], "uv", perm))
    return jnp.stack(pieces)


def per_device(visibility, anchor, offset, slot_rows, counts):
    time_groups = lax.axis_size("tm")
    uv_size = lax.axis_size("uv")
    cell_share = TS * TS // time_groups
    vis_rows = visibility[0]
    row_count, row_width = vis_rows.shape
    tile_count, slot_depth = slot_rows.shape[2:]
    slot_size = tile_count * slot_depth
    lanes = max(row_count, slot_depth, tile_count)
    pad = lambda x: jnp.pad(x, ((0, 0), (0, lanes - x.shape[1])))
    (ints,) = lax.optimization_barrier(
        (
            jnp.concatenate(
                [pad(slot_rows[0, 0]), pad(counts[0]), pad(anchor), pad(offset)], axis=0
            ),
        )
    )
    slot_table = ints[:tile_count, :slot_depth]
    live_count = ints[tile_count, :tile_count]
    anchor_row = ints[tile_count + 1, :row_count]
    offset_row = ints[tile_count + 2, :row_count]
    if uv_size <= 16:
        uv_index = lax.axis_index("uv")
        slot_table = lax.dynamic_slice_in_dim(
            jnp.concatenate([slot_table, slot_table], axis=0), uv_index, tile_count, 0
        )
        live_count = lax.dynamic_slice_in_dim(
            jnp.concatenate([live_count, live_count], axis=0), uv_index, tile_count, 0
        )
    is_live = (jnp.arange(slot_depth, dtype=jnp.int32)[None, :] < live_count[:, None]).reshape(-1)
    flat_index = slot_table.reshape(-1)
    pick = (
        (flat_index[:, None] == jnp.arange(row_count, dtype=jnp.int32)[None, :]) & is_live[:, None]
    ).astype(jnp.bfloat16)
    picked = jnp.dot(pick, vis_rows, preferred_element_type=jnp.float32).astype(jnp.bfloat16)
    meta_rows = jnp.concatenate(
        [anchor_row[None, :], offset_row[None, :], jnp.zeros((META - 2, row_count), jnp.int32)],
        axis=0,
    ).astype(jnp.bfloat16)
    meta = lax.dot_general(
        pick, meta_rows, (((1,), (1,)), ((), ())), preferred_element_type=jnp.float32
    ).astype(jnp.bfloat16)
    outgoing = jnp.concatenate([picked, meta], axis=1).reshape(tile_count, slot_depth, row_width + META)
    arrived = uv_exchange(outgoing, uv_size)
    arrived = arrived.reshape(-1, row_width + META)
    arr_anchor = arrived[:, row_width].astype(jnp.int32)
    arr_offset = arrived[:, row_width + 1].astype(jnp.int32)
    tm_index = lax.axis_index("tm")
    pow2 = time_groups & (time_groups - 1) == 0
    if pow2:
        cells = halving_order(tm_index, time_groups, cell_share)
    else:
        cells = jnp.arange(TS * TS, dtype=jnp.int32)
    weights = tap_matrix(cells, arr_anchor, arr_offset)
    partial = jnp.dot(weights, arrived[:, :row_width], preferred_element_type=jnp.float32)
    if pow2:
        summed = halving_reduce(partial, time_groups)
    else:
        summed = lax.psum_scatter(partial, "tm", scatter_dimension=0, tiled=True)
    grid = summed.astype(jnp.bfloat16)
    out_scale = 4.0 / math.sqrt(NCH * time_groups * ROWS_DEV)
    return jnp.dot(grid, delay_halves(), preferred_element_type=jnp.float32) * out_scale


def solution(mesh):
    in_specs = (
        P("tm", "uv", None),
        P("tm", "uv"),
        P("tm", "uv"),
        P("tm", "uv", None, None),
        P("tm", "uv", None),
    )
    out_specs = P(("uv", "tm"), None)
    return jax.shard_map(
        per_device, mesh=mesh, in_specs=in_specs, out_specs=out_specs, check_vma=False
    )
```

```python
import math

import jax
import jax.numpy as jnp
from jax import lax
from jax.sharding import PartitionSpec as P

NCH = 1024
ROWS_DEV = 128
TS = 16
KTAPS = 8
OSAMP = 8
META = 128
SPLIT = 32


def kernel_taps(offsets):
    tap_index = jnp.arange(KTAPS, dtype=jnp.float32)
    sub_shift = (offsets.astype(jnp.float32) + 0.5) / OSAMP
    distance = tap_index[None, :] - (KTAPS / 2 - 1.0) - sub_shift[:, None]
    return jnp.exp(-distance * distance / (2.0 * 1.2 * 1.2))


def tap_matrix(cell_ids, anchors, offsets):
    span = TS - KTAPS + 1
    anchor_y = anchors // span
    anchor_x = anchors % span
    taps_y = kernel_taps(offsets // OSAMP)
    taps_x = kernel_taps(offsets % OSAMP)
    cell_y = cell_ids // TS
    cell_x = cell_ids % TS
    along_y = jnp.zeros((cell_ids.shape[0], anchors.shape[0]), jnp.float32)
    along_x = jnp.zeros((cell_ids.shape[0], anchors.shape[0]), jnp.float32)
    for step in range(KTAPS):
        along_y = along_y + jnp.where(
            cell_y[:, None] == anchor_y[None, :] + step, taps_y[None, :, step], 0.0
        )
        along_x = along_x + jnp.where(
            cell_x[:, None] == anchor_x[None, :] + step, taps_x[None, :, step], 0.0
        )
    return (along_y * along_x).astype(jnp.bfloat16)


def delay_halves(freq):
    hi = jnp.arange(NCH // SPLIT, dtype=jnp.int32)
    lo = jnp.arange(SPLIT, dtype=jnp.int32)
    scale = 2.0 * math.pi / NCH
    ang_hi = scale * ((freq[:, None] * (SPLIT * hi)[None, :]) % NCH).astype(jnp.float32)
    ang_lo = scale * ((freq[:, None] * lo[None, :]) % NCH).astype(jnp.float32)
    c_hi, s_hi = jnp.cos(ang_hi), jnp.sin(ang_hi)
    c_lo, s_lo = jnp.cos(ang_lo), jnp.sin(ang_lo)
    cosine = c_hi[:, :, None] * c_lo[:, None, :] - s_hi[:, :, None] * s_lo[:, None, :]
    sine = s_hi[:, :, None] * c_lo[:, None, :] + c_hi[:, :, None] * s_lo[:, None, :]
    window_arg = 2.0 * math.pi * freq.astype(jnp.float32) / (NCH - 1)
    taper = (
        0.35875
        - 0.48829 * jnp.cos(window_arg)
        + 0.14128 * jnp.cos(2.0 * window_arg)
        - 0.01168 * jnp.cos(3.0 * window_arg)
    )
    tap_cos = (taper[:, None, None] * cosine).reshape(NCH, NCH)
    tap_sin = (taper[:, None, None] * sine).reshape(NCH, NCH)
    return jnp.concatenate([tap_cos, tap_sin], axis=0).astype(jnp.bfloat16)


def halving_order(tm_index, time_groups, cell_share):
    level_bits = int(math.log2(time_groups))
    quarter = jnp.zeros((time_groups,), jnp.int32)
    for j in range(time_groups):
        value = tm_index
        pos = j
        for level in range(level_bits):
            half = time_groups >> (level + 1)
            sent = pos < half
            bit = 1 << level
            value = jnp.where(sent, value ^ bit, value)
            pos = pos % half if half > 0 else pos
        quarter = quarter.at[j].set(value)
    cells = quarter[:, None] * cell_share + jnp.arange(cell_share, dtype=jnp.int32)[None, :]
    return cells.reshape(-1)


def halving_reduce(partial, time_groups, gated=None):
    level_bits = int(math.log2(time_groups))
    for level in range(level_bits):
        if level == 1 and gated is not None:
            partial, gated = lax.optimization_barrier((partial, gated))
        half = partial.shape[0] // 2
        bit = 1 << level
        perm = [(i, i ^ bit) for i in range(time_groups)]
        outgoing = partial[:half].astype(jnp.bfloat16)
        received = lax.ppermute(outgoing, "tm", perm)
        partial = partial[half:] + received.astype(jnp.float32)
    return partial, gated


def uv_exchange(outgoing, uv_size):
    if uv_size > 16:
        return lax.all_to_all(outgoing, "uv", split_axis=0, concat_axis=0, tiled=True)
    pieces = [outgoing[0]]
    for shift in range(1, uv_size):
        perm = [(i, (i + shift) % uv_size) for i in range(uv_size)]
        pieces.append(lax.ppermute(outgoing[shift], "uv", perm))
    return jnp.stack(pieces)


def per_device(visibility, anchor, offset, slot_rows, counts):
    time_groups = lax.axis_size("tm")
    uv_size = lax.axis_size("uv")
    cell_share = TS * TS // time_groups
    vis_rows = visibility[0]
    row_count, row_width = vis_rows.shape
    tile_count, slot_depth = slot_rows.shape[2:]
    slot_size = tile_count * slot_depth
    lanes = max(row_count, slot_depth, tile_count)
    pad = lambda x: jnp.pad(x, ((0, 0), (0, lanes - x.shape[1])))
    (ints,) = lax.optimization_barrier(
        (
            jnp.concatenate(
                [pad(slot_rows[0, 0]), pad(counts[0]), pad(anchor), pad(offset)], axis=0
            ),
        )
    )
    slot_table = ints[:tile_count, :slot_depth]
    live_count = ints[tile_count, :tile_count]
    anchor_row = ints[tile_count + 1, :row_count]
    offset_row = ints[tile_count + 2, :row_count]
    if uv_size <= 16:
        uv_index = lax.axis_index("uv")
        slot_table = lax.dynamic_slice_in_dim(
            jnp.concatenate([slot_table, slot_table], axis=0), uv_index, tile_count, 0
        )
        live_count = lax.dynamic_slice_in_dim(
            jnp.concatenate([live_count, live_count], axis=0), uv_index, tile_count, 0
        )
    is_live = (jnp.arange(slot_depth, dtype=jnp.int32)[None, :] < live_count[:, None]).reshape(-1)
    flat_index = slot_table.reshape(-1)
    pick = (
        (flat_index[:, None] == jnp.arange(row_count, dtype=jnp.int32)[None, :]) & is_live[:, None]
    ).astype(jnp.bfloat16)
    picked = jnp.dot(pick, vis_rows, preferred_element_type=jnp.float32).astype(jnp.bfloat16)
    meta_rows = jnp.concatenate(
        [anchor_row[None, :], offset_row[None, :], jnp.zeros((META - 2, row_count), jnp.int32)],
        axis=0,
    ).astype(jnp.bfloat16)
    meta = lax.dot_general(
        pick, meta_rows, (((1,), (1,)), ((), ())), preferred_element_type=jnp.float32
    ).astype(jnp.bfloat16)
    outgoing = jnp.concatenate([picked, meta], axis=1).reshape(tile_count, slot_depth, row_width + META)
    arrived = uv_exchange(outgoing, uv_size)
    arrived = arrived.reshape(-1, row_width + META)
    arr_anchor = arrived[:, row_width].astype(jnp.int32)
    arr_offset = arrived[:, row_width + 1].astype(jnp.int32)
    tm_index = lax.axis_index("tm")
    pow2 = time_groups & (time_groups - 1) == 0
    if pow2:
        cells = halving_order(tm_index, time_groups, cell_share)
    else:
        cells = jnp.arange(TS * TS, dtype=jnp.int32)
    weights = tap_matrix(cells, arr_anchor, arr_offset)
    partial = jnp.dot(weights, arrived[:, :row_width], preferred_element_type=jnp.float32)
    freq = jnp.arange(NCH, dtype=jnp.int32)
    if pow2 and time_groups > 2:
        summed, freq = halving_reduce(partial, time_groups, freq)
    elif pow2:
        summed, _ = halving_reduce(partial, time_groups)
    else:
        summed = lax.psum_scatter(partial, "tm", scatter_dimension=0, tiled=True)
    grid = summed.astype(jnp.bfloat16)
    grid_re, grid_im = grid[:, :NCH], grid[:, NCH:]
    lhs = jnp.concatenate(
        [grid, jnp.concatenate([grid_im, -grid_re], axis=1)], axis=0
    )
    out_scale = 4.0 / math.sqrt(NCH * time_groups * ROWS_DEV)
    both = jnp.dot(lhs, delay_halves(freq), preferred_element_type=jnp.float32) * out_scale
    cells_out = grid.shape[0]
    return jnp.concatenate([both[:cells_out], both[cells_out:]], axis=1)


def solution(mesh):
    in_specs = (
        P("tm", "uv", None),
        P("tm", "uv"),
        P("tm", "uv"),
        P("tm", "uv", None, None),
        P("tm", "uv", None),
    )
    out_specs = P(("uv", "tm"), None)
    return jax.shard_map(
        per_device, mesh=mesh, in_specs=in_specs, out_specs=out_specs, check_vma=False
    )
```

```python
import math

import jax
import jax.numpy as jnp
from jax import lax
from jax.experimental import pallas as pl
from jax.sharding import PartitionSpec as P

NCH = 1024
ROWS_DEV = 128
TS = 16
KTAPS = 8
OSAMP = 8
META = 128
SPLIT = 32


def kernel_taps(offsets):
    tap_index = jnp.arange(KTAPS, dtype=jnp.float32)
    sub_shift = (offsets.astype(jnp.float32) + 0.5) / OSAMP
    distance = tap_index[None, :] - (KTAPS / 2 - 1.0) - sub_shift[:, None]
    return jnp.exp(-distance * distance / (2.0 * 1.2 * 1.2))


def tap_matrix(cell_ids, anchors, offsets):
    span = TS - KTAPS + 1
    anchor_y = anchors // span
    anchor_x = anchors % span
    taps_y = kernel_taps(offsets // OSAMP)
    taps_x = kernel_taps(offsets % OSAMP)
    cell_y = cell_ids // TS
    cell_x = cell_ids % TS
    along_y = jnp.zeros((cell_ids.shape[0], anchors.shape[0]), jnp.float32)
    along_x = jnp.zeros((cell_ids.shape[0], anchors.shape[0]), jnp.float32)
    for step in range(KTAPS):
        along_y = along_y + jnp.where(
            cell_y[:, None] == anchor_y[None, :] + step, taps_y[None, :, step], 0.0
        )
        along_x = along_x + jnp.where(
            cell_x[:, None] == anchor_x[None, :] + step, taps_x[None, :, step], 0.0
        )
    return (along_y * along_x).astype(jnp.bfloat16)


def delay_halves():
    freq = jnp.arange(NCH, dtype=jnp.int32)
    hi = jnp.arange(NCH // SPLIT, dtype=jnp.int32)
    lo = jnp.arange(SPLIT, dtype=jnp.int32)
    scale = 2.0 * math.pi / NCH
    ang_hi = scale * ((freq[:, None] * (SPLIT * hi)[None, :]) % NCH).astype(jnp.float32)
    ang_lo = scale * ((freq[:, None] * lo[None, :]) % NCH).astype(jnp.float32)
    c_hi, s_hi = jnp.cos(ang_hi), jnp.sin(ang_hi)
    c_lo, s_lo = jnp.cos(ang_lo), jnp.sin(ang_lo)
    cosine = c_hi[:, :, None] * c_lo[:, None, :] - s_hi[:, :, None] * s_lo[:, None, :]
    sine = s_hi[:, :, None] * c_lo[:, None, :] + c_hi[:, :, None] * s_lo[:, None, :]
    window_arg = 2.0 * math.pi * freq.astype(jnp.float32) / (NCH - 1)
    taper = (
        0.35875
        - 0.48829 * jnp.cos(window_arg)
        + 0.14128 * jnp.cos(2.0 * window_arg)
        - 0.01168 * jnp.cos(3.0 * window_arg)
    )
    tap_cos = (taper[:, None, None] * cosine).reshape(NCH, NCH)
    tap_sin = (taper[:, None, None] * sine).reshape(NCH, NCH)
    return jnp.concatenate([tap_cos, tap_sin], axis=0).astype(jnp.bfloat16)


def final_transform(grid, halves, scale):
    cells = grid.shape[0]
    half = halves.shape[1]

    def kernel(g_ref, h_ref, o_ref):
        grid_re = g_ref[:, :half]
        grid_im = g_ref[:, half:]
        tap_cos = h_ref[:half, :]
        tap_sin = h_ref[half:, :]
        real = jnp.dot(grid_re, tap_cos, preferred_element_type=jnp.float32) + jnp.dot(
            grid_im, tap_sin, preferred_element_type=jnp.float32
        )
        imag = jnp.dot(grid_im, tap_cos, preferred_element_type=jnp.float32) - jnp.dot(
            grid_re, tap_sin, preferred_element_type=jnp.float32
        )
        o_ref[:, :half] = real * scale
        o_ref[:, half:] = imag * scale

    return pl.pallas_call(
        kernel, out_shape=jax.ShapeDtypeStruct((cells, 2 * half), jnp.float32)
    )(grid, halves)


def halving_order(tm_index, time_groups, cell_share):
    level_bits = int(math.log2(time_groups))
    quarter = jnp.zeros((time_groups,), jnp.int32)
    for j in range(time_groups):
        value = tm_index
        pos = j
        for level in range(level_bits):
            half = time_groups >> (level + 1)
            sent = pos < half
            bit = 1 << level
            value = jnp.where(sent, value ^ bit, value)
            pos = pos % half if half > 0 else pos
        quarter = quarter.at[j].set(value)
    cells = quarter[:, None] * cell_share + jnp.arange(cell_share, dtype=jnp.int32)[None, :]
    return cells.reshape(-1)


def halving_reduce(partial, time_groups):
    level_bits = int(math.log2(time_groups))
    for level in range(level_bits):
        half = partial.shape[0] // 2
        bit = 1 << level
        perm = [(i, i ^ bit) for i in range(time_groups)]
        outgoing = partial[:half]
        if level > 0:
            outgoing = outgoing.astype(jnp.bfloat16)
        received = lax.ppermute(outgoing, "tm", perm)
        partial = partial[half:] + received.astype(jnp.float32)
    return partial


def uv_exchange(outgoing, uv_size):
    if uv_size > 16:
        return lax.all_to_all(outgoing, "uv", split_axis=0, concat_axis=0, tiled=True)
    pieces = [outgoing[0]]
    for shift in range(1, uv_size):
        perm = [(i, (i + shift) % uv_size) for i in range(uv_size)]
        pieces.append(lax.ppermute(outgoing[shift], "uv", perm))
    return jnp.stack(pieces)


def per_device(visibility, anchor, offset, slot_rows, counts):
    time_groups = lax.axis_size("tm")
    uv_size = lax.axis_size("uv")
    cell_share = TS * TS // time_groups
    vis_rows = visibility[0]
    row_count, row_width = vis_rows.shape
    tile_count, slot_depth = slot_rows.shape[2:]
    slot_size = tile_count * slot_depth
    lanes = max(row_count, slot_depth, tile_count)
    pad = lambda x: jnp.pad(x, ((0, 0), (0, lanes - x.shape[1])))
    (ints,) = lax.optimization_barrier(
        (
            jnp.concatenate(
                [pad(slot_rows[0, 0]), pad(counts[0]), pad(anchor), pad(offset)], axis=0
            ),
        )
    )
    slot_table = ints[:tile_count, :slot_depth]
    live_count = ints[tile_count, :tile_count]
    anchor_row = ints[tile_count + 1, :row_count]
    offset_row = ints[tile_count + 2, :row_count]
    if uv_size <= 16:
        uv_index = lax.axis_index("uv")
        slot_table = lax.dynamic_slice_in_dim(
            jnp.concatenate([slot_table, slot_table], axis=0), uv_index, tile_count, 0
        )
        live_count = lax.dynamic_slice_in_dim(
            jnp.concatenate([live_count, live_count], axis=0), uv_index, tile_count, 0
        )
    is_live = (jnp.arange(slot_depth, dtype=jnp.int32)[None, :] < live_count[:, None]).reshape(-1)
    flat_index = slot_table.reshape(-1)
    pick = (
        (flat_index[:, None] == jnp.arange(row_count, dtype=jnp.int32)[None, :]) & is_live[:, None]
    ).astype(jnp.bfloat16)
    picked = jnp.dot(pick, vis_rows, preferred_element_type=jnp.float32).astype(jnp.bfloat16)
    meta_rows = jnp.concatenate(
        [anchor_row[None, :], offset_row[None, :], jnp.zeros((META - 2, row_count), jnp.int32)],
        axis=0,
    ).astype(jnp.bfloat16)
    meta = lax.dot_general(
        pick, meta_rows, (((1,), (1,)), ((), ())), preferred_element_type=jnp.float32
    ).astype(jnp.bfloat16)
    outgoing = jnp.concatenate([picked, meta], axis=1).reshape(tile_count, slot_depth, row_width + META)
    arrived = uv_exchange(outgoing, uv_size)
    arrived = arrived.reshape(-1, row_width + META)
    arr_anchor = arrived[:, row_width].astype(jnp.int32)
    arr_offset = arrived[:, row_width + 1].astype(jnp.int32)
    tm_index = lax.axis_index("tm")
    pow2 = time_groups & (time_groups - 1) == 0
    if pow2:
        cells = halving_order(tm_index, time_groups, cell_share)
    else:
        cells = jnp.arange(TS * TS, dtype=jnp.int32)
    weights = tap_matrix(cells, arr_anchor, arr_offset)
    partial = jnp.dot(weights, arrived[:, :row_width], preferred_element_type=jnp.float32)
    if pow2:
        summed = halving_reduce(partial, time_groups)
    else:
        summed = lax.psum_scatter(partial, "tm", scatter_dimension=0, tiled=True)
    grid = summed.astype(jnp.bfloat16)
    out_scale = 4.0 / math.sqrt(NCH * time_groups * ROWS_DEV)
    return final_transform(grid, delay_halves(), out_scale)


def solution(mesh):
    in_specs = (
        P("tm", "uv", None),
        P("tm", "uv"),
        P("tm", "uv"),
        P("tm", "uv", None, None),
        P("tm", "uv", None),
    )
    out_specs = P(("uv", "tm"), None)
    return jax.shard_map(
        per_device, mesh=mesh, in_specs=in_specs, out_specs=out_specs, check_vma=False
    )
```

```python
import math

import jax
import jax.numpy as jnp
from jax import lax
from jax.sharding import PartitionSpec as P

NCH = 1024
ROWS_DEV = 128
TS = 16
KTAPS = 8
OSAMP = 8
META = 128
SPLIT = 32


def kernel_taps(offsets):
    tap_index = jnp.arange(KTAPS, dtype=jnp.float32)
    sub_shift = (offsets.astype(jnp.float32) + 0.5) / OSAMP
    distance = tap_index[None, :] - (KTAPS / 2 - 1.0) - sub_shift[:, None]
    return jnp.exp(-distance * distance / (2.0 * 1.2 * 1.2))


def tap_matrix(cell_ids, anchors, offsets):
    span = TS - KTAPS + 1
    anchor_y = anchors // span
    anchor_x = anchors % span
    taps_y = kernel_taps(offsets // OSAMP)
    taps_x = kernel_taps(offsets % OSAMP)
    cell_y = cell_ids // TS
    cell_x = cell_ids % TS
    along_y = jnp.zeros((cell_ids.shape[0], anchors.shape[0]), jnp.float32)
    along_x = jnp.zeros((cell_ids.shape[0], anchors.shape[0]), jnp.float32)
    for step in range(KTAPS):
        along_y = along_y + jnp.where(
            cell_y[:, None] == anchor_y[None, :] + step, taps_y[None, :, step], 0.0
        )
        along_x = along_x + jnp.where(
            cell_x[:, None] == anchor_x[None, :] + step, taps_x[None, :, step], 0.0
        )
    return (along_y * along_x).astype(jnp.bfloat16)


def delay_halves():
    freq = jnp.arange(NCH, dtype=jnp.int32)
    hi = jnp.arange(NCH // SPLIT, dtype=jnp.int32)
    lo = jnp.arange(SPLIT, dtype=jnp.int32)
    scale = 2.0 * math.pi / NCH
    ang_hi = scale * ((freq[:, None] * (SPLIT * hi)[None, :]) % NCH).astype(jnp.float32)
    ang_lo = scale * ((freq[:, None] * lo[None, :]) % NCH).astype(jnp.float32)
    c_hi, s_hi = jnp.cos(ang_hi), jnp.sin(ang_hi)
    c_lo, s_lo = jnp.cos(ang_lo), jnp.sin(ang_lo)
    cosine = c_hi[:, :, None] * c_lo[:, None, :] - s_hi[:, :, None] * s_lo[:, None, :]
    sine = s_hi[:, :, None] * c_lo[:, None, :] + c_hi[:, :, None] * s_lo[:, None, :]
    window_arg = 2.0 * math.pi * freq.astype(jnp.float32) / (NCH - 1)
    taper = (
        0.35875
        - 0.48829 * jnp.cos(window_arg)
        + 0.14128 * jnp.cos(2.0 * window_arg)
        - 0.01168 * jnp.cos(3.0 * window_arg)
    )
    tap_cos = (taper[:, None, None] * cosine).reshape(NCH, NCH)
    tap_sin = (taper[:, None, None] * sine).reshape(NCH, NCH)
    return jnp.concatenate([tap_cos, tap_sin], axis=0).astype(jnp.bfloat16)


def halving_order(tm_index, time_groups, cell_share):
    level_bits = int(math.log2(time_groups))
    quarter = jnp.zeros((time_groups,), jnp.int32)
    for j in range(time_groups):
        value = tm_index
        pos = j
        for level in range(level_bits):
            half = time_groups >> (level + 1)
            sent = pos < half
            bit = 1 << level
            value = jnp.where(sent, value ^ bit, value)
            pos = pos % half if half > 0 else pos
        quarter = quarter.at[j].set(value)
    cells = quarter[:, None] * cell_share + jnp.arange(cell_share, dtype=jnp.int32)[None, :]
    return cells.reshape(-1)


def halving_reduce(partial, time_groups):
    level_bits = int(math.log2(time_groups))
    for level in range(level_bits):
        half = partial.shape[0] // 2
        bit = 1 << level
        perm = [(i, i ^ bit) for i in range(time_groups)]
        outgoing = partial[:half]
        if level > 0:
            outgoing = outgoing.astype(jnp.bfloat16)
        received = lax.ppermute(outgoing, "tm", perm)
        partial = partial[half:] + received.astype(jnp.float32)
    return partial


def uv_exchange(outgoing, uv_size):
    if uv_size > 16:
        return lax.all_to_all(outgoing, "uv", split_axis=0, concat_axis=0, tiled=True)
    pieces = [outgoing[0]]
    for shift in range(1, uv_size):
        perm = [(i, (i + shift) % uv_size) for i in range(uv_size)]
        pieces.append(lax.ppermute(outgoing[shift], "uv", perm))
    return jnp.stack(pieces)


def per_device(visibility, anchor, offset, slot_rows, counts):
    time_groups = lax.axis_size("tm")
    uv_size = lax.axis_size("uv")
    cell_share = TS * TS // time_groups
    vis_rows = visibility[0]
    row_count, row_width = vis_rows.shape
    tile_count, slot_depth = slot_rows.shape[2:]
    slot_size = tile_count * slot_depth
    lanes = max(row_count, slot_depth, tile_count)
    pad = lambda x: jnp.pad(x, ((0, 0), (0, lanes - x.shape[1])))
    (ints,) = lax.optimization_barrier(
        (
            jnp.concatenate(
                [pad(slot_rows[0, 0]), pad(counts[0]), pad(anchor), pad(offset)], axis=0
            ),
        )
    )
    slot_table = ints[:tile_count, :slot_depth]
    live_count = ints[tile_count, :tile_count]
    anchor_row = ints[tile_count + 1, :row_count]
    offset_row = ints[tile_count + 2, :row_count]
    if uv_size <= 16:
        uv_index = lax.axis_index("uv")
        slot_table = lax.dynamic_slice_in_dim(
            jnp.concatenate([slot_table, slot_table], axis=0), uv_index, tile_count, 0
        )
        live_count = lax.dynamic_slice_in_dim(
            jnp.concatenate([live_count, live_count], axis=0), uv_index, tile_count, 0
        )
    is_live = jnp.arange(slot_depth, dtype=jnp.int32)[None, :] < live_count[:, None]
    pair_index = slot_table.reshape(-1, 2)
    pair_live = is_live.reshape(-1, 2)
    rows_iota = jnp.arange(row_count, dtype=jnp.int32)[None, :]
    picks = [
        ((pair_index[:, h:h + 1] == rows_iota) & pair_live[:, h:h + 1]).astype(jnp.bfloat16)
        for h in range(2)
    ]
    picked = [
        jnp.dot(pick, vis_rows, preferred_element_type=jnp.float32).astype(jnp.bfloat16)
        for pick in picks
    ]
    zero_rows = jnp.zeros((2, row_count), jnp.int32)
    meta_rows = jnp.concatenate(
        [
            jnp.concatenate(
                [anchor_row[None, :], offset_row[None, :], zero_rows,
                 jnp.zeros((META - 4, row_count), jnp.int32)], axis=0
            ),
            jnp.concatenate(
                [zero_rows, anchor_row[None, :], offset_row[None, :],
                 jnp.zeros((META - 4, row_count), jnp.int32)], axis=0
            ),
        ],
        axis=1,
    ).astype(jnp.bfloat16)
    meta = lax.dot_general(
        jnp.concatenate(picks, axis=1), meta_rows, (((1,), (1,)), ((), ())),
        preferred_element_type=jnp.float32,
    ).astype(jnp.bfloat16)
    pair_depth = slot_depth // 2
    width = 2 * row_width + META
    outgoing = jnp.concatenate(picked + [meta], axis=1).reshape(tile_count, pair_depth, width)
    arrived = uv_exchange(outgoing, uv_size)
    arrived = arrived.reshape(-1, width)
    tm_index = lax.axis_index("tm")
    pow2 = time_groups & (time_groups - 1) == 0
    if pow2:
        cells = halving_order(tm_index, time_groups, cell_share)
    else:
        cells = jnp.arange(TS * TS, dtype=jnp.int32)
    partial = None
    for h in range(2):
        arr_anchor = arrived[:, 2 * row_width + 2 * h].astype(jnp.int32)
        arr_offset = arrived[:, 2 * row_width + 2 * h + 1].astype(jnp.int32)
        weights = tap_matrix(cells, arr_anchor, arr_offset)
        part = jnp.dot(
            weights, arrived[:, h * row_width:(h + 1) * row_width], preferred_element_type=jnp.float32
        )
        partial = part if partial is None else partial + part
    if pow2:
        summed = halving_reduce(partial, time_groups)
    else:
        summed = lax.psum_scatter(partial, "tm", scatter_dimension=0, tiled=True)
    grid = summed.astype(jnp.bfloat16)
    grid_re, grid_im = grid[:, :NCH], grid[:, NCH:]
    lhs = jnp.concatenate(
        [grid, jnp.concatenate([grid_im, -grid_re], axis=1)], axis=0
    )
    out_scale = 4.0 / math.sqrt(NCH * time_groups * ROWS_DEV)
    both = jnp.dot(lhs, delay_halves(), preferred_element_type=jnp.float32) * out_scale
    cells_out = grid.shape[0]
    return jnp.concatenate([both[:cells_out], both[cells_out:]], axis=1)


def solution(mesh):
    in_specs = (
        P("tm", "uv", None),
        P("tm", "uv"),
        P("tm", "uv"),
        P("tm", "uv", None, None),
        P("tm", "uv", None),
    )
    out_specs = P(("uv", "tm"), None)
    return jax.shard_map(
        per_device, mesh=mesh, in_specs=in_specs, out_specs=out_specs, check_vma=False
    )
```

```python
import math

import jax
import jax.numpy as jnp
from jax import lax
from jax.sharding import PartitionSpec as P

NCH = 1024
ROWS_DEV = 128
TS = 16
KTAPS = 8
OSAMP = 8
META = 128
SPLIT = 32


def kernel_taps(offsets):
    tap_index = jnp.arange(KTAPS, dtype=jnp.float32)
    sub_shift = (offsets.astype(jnp.float32) + 0.5) / OSAMP
    distance = tap_index[None, :] - (KTAPS / 2 - 1.0) - sub_shift[:, None]
    return jnp.exp(-distance * distance / (2.0 * 1.2 * 1.2))


def tap_matrix(cell_ids, anchors, offsets):
    span = TS - KTAPS + 1
    anchor_y = anchors // span
    anchor_x = anchors % span
    taps_y = kernel_taps(offsets // OSAMP)
    taps_x = kernel_taps(offsets % OSAMP)
    cell_y = cell_ids // TS
    cell_x = cell_ids % TS
    along_y = jnp.zeros((cell_ids.shape[0], anchors.shape[0]), jnp.float32)
    along_x = jnp.zeros((cell_ids.shape[0], anchors.shape[0]), jnp.float32)
    for step in range(KTAPS):
        along_y = along_y + jnp.where(
            cell_y[:, None] == anchor_y[None, :] + step, taps_y[None, :, step], 0.0
        )
        along_x = along_x + jnp.where(
            cell_x[:, None] == anchor_x[None, :] + step, taps_x[None, :, step], 0.0
        )
    return (along_y * along_x).astype(jnp.bfloat16)


def delay_halves():
    freq = jnp.arange(NCH, dtype=jnp.int32)
    hi = jnp.arange(NCH // SPLIT, dtype=jnp.int32)
    lo = jnp.arange(SPLIT, dtype=jnp.int32)
    scale = 2.0 * math.pi / NCH
    ang_hi = scale * ((freq[:, None] * (SPLIT * hi)[None, :]) % NCH).astype(jnp.float32)
    ang_lo = scale * ((freq[:, None] * lo[None, :]) % NCH).astype(jnp.float32)
    c_hi, s_hi = jnp.cos(ang_hi), jnp.sin(ang_hi)
    c_lo, s_lo = jnp.cos(ang_lo), jnp.sin(ang_lo)
    cosine = c_hi[:, :, None] * c_lo[:, None, :] - s_hi[:, :, None] * s_lo[:, None, :]
    sine = s_hi[:, :, None] * c_lo[:, None, :] + c_hi[:, :, None] * s_lo[:, None, :]
    window_arg = 2.0 * math.pi * freq.astype(jnp.float32) / (NCH - 1)
    taper = (
        0.35875
        - 0.48829 * jnp.cos(window_arg)
        + 0.14128 * jnp.cos(2.0 * window_arg)
        - 0.01168 * jnp.cos(3.0 * window_arg)
    )
    tap_cos = (taper[:, None, None] * cosine).reshape(NCH, NCH)
    tap_sin = (taper[:, None, None] * sine).reshape(NCH, NCH)
    return jnp.concatenate([tap_cos, tap_sin], axis=0).astype(jnp.bfloat16)


def halving_order(tm_index, time_groups, cell_share):
    level_bits = int(math.log2(time_groups))
    quarter = jnp.zeros((time_groups,), jnp.int32)
    for j in range(time_groups):
        value = tm_index
        pos = j
        for level in range(level_bits):
            half = time_groups >> (level + 1)
            sent = pos < half
            bit = 1 << level
            value = jnp.where(sent, value ^ bit, value)
            pos = pos % half if half > 0 else pos
        quarter = quarter.at[j].set(value)
    cells = quarter[:, None] * cell_share + jnp.arange(cell_share, dtype=jnp.int32)[None, :]
    return cells.reshape(-1)


def halving_reduce(partial, time_groups):
    level_bits = int(math.log2(time_groups))
    for level in range(level_bits):
        half = partial.shape[0] // 2
        bit = 1 << level
        perm = [(i, i ^ bit) for i in range(time_groups)]
        outgoing = partial[:half]
        if level > 0:
            outgoing = outgoing.astype(jnp.bfloat16)
        received = lax.ppermute(outgoing, "tm", perm)
        partial = partial[half:] + received.astype(jnp.float32)
    return partial


def uv_exchange(outgoing, uv_size, tm_size):
    if uv_size > 16:
        return lax.all_to_all(outgoing, "uv", split_axis=0, concat_axis=0, tiled=True)
    if tm_size % 2:
        pieces = [outgoing[0]]
        for shift in range(1, uv_size):
            perm = [(i, (i + shift) % uv_size) for i in range(uv_size)]
            pieces.append(lax.ppermute(outgoing[shift], "uv", perm))
        return jnp.stack(pieces)
    shifts = list(range(1, uv_size))
    count = (len(shifts) + 1) // 2
    sets = [shifts[:count], shifts[count:] + [None] * (2 * count - len(shifts))]
    zero = jnp.zeros(outgoing.shape[1:], outgoing.dtype)
    stacks = [jnp.stack([outgoing[k] if k else zero for k in group]) for group in sets]
    side = lax.axis_index("tm") % 2
    mine = jnp.where(side == 0, stacks[0], stacks[1])
    theirs = jnp.where(side == 0, stacks[1], stacks[0])
    pair_perm = [(i, i ^ 1) for i in range(tm_size)]
    partner = lax.ppermute(theirs, "tm", pair_perm)
    kept, passed = [], []
    for j in range(count):
        perm = []
        for u in range(uv_size):
            for t in range(tm_size):
                shift = sets[t % 2][j]
                if shift:
                    perm.append((u * tm_size + t, ((u + shift) % uv_size) * tm_size + t))
        got = lax.ppermute(jnp.stack([mine[j], partner[j]]), ("uv", "tm"), perm)
        kept.append(got[0])
        passed.append(got[1])
    forwarded = lax.ppermute(jnp.stack(passed), "tm", pair_perm)
    return jnp.concatenate([outgoing[:1], jnp.stack(kept), forwarded], axis=0)


def per_device(visibility, anchor, offset, slot_rows, counts):
    time_groups = lax.axis_size("tm")
    uv_size = lax.axis_size("uv")
    cell_share = TS * TS // time_groups
    vis_rows = visibility[0]
    row_count, row_width = vis_rows.shape
    tile_count, slot_depth = slot_rows.shape[2:]
    slot_size = tile_count * slot_depth
    lanes = max(row_count, slot_depth, tile_count)
    pad = lambda x: jnp.pad(x, ((0, 0), (0, lanes - x.shape[1])))
    (ints,) = lax.optimization_barrier(
        (
            jnp.concatenate(
                [pad(slot_rows[0, 0]), pad(counts[0]), pad(anchor), pad(offset)], axis=0
            ),
        )
    )
    slot_table = ints[:tile_count, :slot_depth]
    live_count = ints[tile_count, :tile_count]
    anchor_row = ints[tile_count + 1, :row_count]
    offset_row = ints[tile_count + 2, :row_count]
    if uv_size <= 16:
        uv_index = lax.axis_index("uv")
        slot_table = lax.dynamic_slice_in_dim(
            jnp.concatenate([slot_table, slot_table], axis=0), uv_index, tile_count, 0
        )
        live_count = lax.dynamic_slice_in_dim(
            jnp.concatenate([live_count, live_count], axis=0), uv_index, tile_count, 0
        )
    is_live = (jnp.arange(slot_depth, dtype=jnp.int32)[None, :] < live_count[:, None]).reshape(-1)
    flat_index = slot_table.reshape(-1)
    pick = (
        (flat_index[:, None] == jnp.arange(row_count, dtype=jnp.int32)[None, :]) & is_live[:, None]
    ).astype(jnp.bfloat16)
    picked = jnp.dot(pick, vis_rows, preferred_element_type=jnp.float32).astype(jnp.bfloat16)
    meta_rows = jnp.concatenate(
        [anchor_row[None, :], offset_row[None, :], jnp.zeros((META - 2, row_count), jnp.int32)],
        axis=0,
    ).astype(jnp.bfloat16)
    meta = lax.dot_general(
        pick, meta_rows, (((1,), (1,)), ((), ())), preferred_element_type=jnp.float32
    ).astype(jnp.bfloat16)
    outgoing = jnp.concatenate([picked, meta], axis=1).reshape(tile_count, slot_depth, row_width + META)
    arrived = uv_exchange(outgoing, uv_size, time_groups)
    arrived = arrived.reshape(-1, row_width + META)
    arr_anchor = arrived[:, row_width].astype(jnp.int32)
    arr_offset = arrived[:, row_width + 1].astype(jnp.int32)
    tm_index = lax.axis_index("tm")
    pow2 = time_groups & (time_groups - 1) == 0
    if pow2:
        cells = halving_order(tm_index, time_groups, cell_share)
    else:
        cells = jnp.arange(TS * TS, dtype=jnp.int32)
    weights = tap_matrix(cells, arr_anchor, arr_offset)
    partial = jnp.dot(weights, arrived[:, :row_width], preferred_element_type=jnp.float32)
    if pow2:
        summed = halving_reduce(partial, time_groups)
    else:
        summed = lax.psum_scatter(partial, "tm", scatter_dimension=0, tiled=True)
    grid = summed.astype(jnp.bfloat16)
    grid_re, grid_im = grid[:, :NCH], grid[:, NCH:]
    lhs = jnp.concatenate(
        [grid, jnp.concatenate([grid_im, -grid_re], axis=1)], axis=0
    )
    out_scale = 4.0 / math.sqrt(NCH * time_groups * ROWS_DEV)
    both = jnp.dot(lhs, delay_halves(), preferred_element_type=jnp.float32) * out_scale
    cells_out = grid.shape[0]
    return jnp.concatenate([both[:cells_out], both[cells_out:]], axis=1)


def solution(mesh):
    in_specs = (
        P("tm", "uv", None),
        P("tm", "uv"),
        P("tm", "uv"),
        P("tm", "uv", None, None),
        P("tm", "uv", None),
    )
    out_specs = P(("uv", "tm"), None)
    return jax.shard_map(
        per_device, mesh=mesh, in_specs=in_specs, out_specs=out_specs, check_vma=False
    )
```

```python
import math

import jax
import jax.numpy as jnp
from jax import lax
from jax.sharding import PartitionSpec as P

NCH = 1024
ROWS_DEV = 128
TS = 16
KTAPS = 8
OSAMP = 8
META = 128
SPLIT = 32


def kernel_taps(offsets):
    tap_index = jnp.arange(KTAPS, dtype=jnp.float32)
    sub_shift = (offsets.astype(jnp.float32) + 0.5) / OSAMP
    distance = tap_index[None, :] - (KTAPS / 2 - 1.0) - sub_shift[:, None]
    return jnp.exp(-distance * distance / (2.0 * 1.2 * 1.2))


def tap_matrix(cell_ids, anchors, offsets):
    span = TS - KTAPS + 1
    anchor_y = anchors // span
    anchor_x = anchors % span
    taps_y = kernel_taps(offsets // OSAMP)
    taps_x = kernel_taps(offsets % OSAMP)
    cell_y = cell_ids // TS
    cell_x = cell_ids % TS
    along_y = jnp.zeros((cell_ids.shape[0], anchors.shape[0]), jnp.float32)
    along_x = jnp.zeros((cell_ids.shape[0], anchors.shape[0]), jnp.float32)
    for step in range(KTAPS):
        along_y = along_y + jnp.where(
            cell_y[:, None] == anchor_y[None, :] + step, taps_y[None, :, step], 0.0
        )
        along_x = along_x + jnp.where(
            cell_x[:, None] == anchor_x[None, :] + step, taps_x[None, :, step], 0.0
        )
    return (along_y * along_x).astype(jnp.bfloat16)


def delay_halves():
    freq = jnp.arange(NCH, dtype=jnp.int32)
    hi = jnp.arange(NCH // SPLIT, dtype=jnp.int32)
    lo = jnp.arange(SPLIT, dtype=jnp.int32)
    scale = 2.0 * math.pi / NCH
    ang_hi = scale * ((freq[:, None] * (SPLIT * hi)[None, :]) % NCH).astype(jnp.float32)
    ang_lo = scale * ((freq[:, None] * lo[None, :]) % NCH).astype(jnp.float32)
    c_hi, s_hi = jnp.cos(ang_hi), jnp.sin(ang_hi)
    c_lo, s_lo = jnp.cos(ang_lo), jnp.sin(ang_lo)
    cosine = c_hi[:, :, None] * c_lo[:, None, :] - s_hi[:, :, None] * s_lo[:, None, :]
    sine = s_hi[:, :, None] * c_lo[:, None, :] + c_hi[:, :, None] * s_lo[:, None, :]
    window_arg = 2.0 * math.pi * freq.astype(jnp.float32) / (NCH - 1)
    taper = (
        0.35875
        - 0.48829 * jnp.cos(window_arg)
        + 0.14128 * jnp.cos(2.0 * window_arg)
        - 0.01168 * jnp.cos(3.0 * window_arg)
    )
    tap_cos = (taper[:, None, None] * cosine).reshape(NCH, NCH)
    tap_sin = (taper[:, None, None] * sine).reshape(NCH, NCH)
    return jnp.concatenate([tap_cos, tap_sin], axis=0).astype(jnp.bfloat16)


def halving_order(tm_index, time_groups, cell_share):
    level_bits = int(math.log2(time_groups))
    quarter = jnp.zeros((time_groups,), jnp.int32)
    for j in range(time_groups):
        value = tm_index
        pos = j
        for level in range(level_bits):
            half = time_groups >> (level + 1)
            sent = pos < half
            bit = 1 << level
            value = jnp.where(sent, value ^ bit, value)
            pos = pos % half if half > 0 else pos
        quarter = quarter.at[j].set(value)
    cells = quarter[:, None] * cell_share + jnp.arange(cell_share, dtype=jnp.int32)[None, :]
    return cells.reshape(-1)


def halving_reduce(partial, time_groups):
    level_bits = int(math.log2(time_groups))
    for level in range(level_bits):
        half = partial.shape[0] // 2
        bit = 1 << level
        perm = [(i, i ^ bit) for i in range(time_groups)]
        outgoing = partial[:half]
        if level > 0:
            outgoing = outgoing.astype(jnp.bfloat16)
        received = lax.ppermute(outgoing, "tm", perm)
        partial = partial[half:] + received.astype(jnp.float32)
    return partial


def uv_exchange(outgoing, uv_size):
    if uv_size > 16:
        return lax.all_to_all(outgoing, "uv", split_axis=0, concat_axis=0, tiled=True)
    pieces = [outgoing[0]]
    half = uv_size // 2
    order = [half] + [k for k in range(2, uv_size, 2) if k != half]
    order += [k for k in range(1, uv_size, 2)]
    for shift in order:
        perm = [(i, (i + shift) % uv_size) for i in range(uv_size)]
        pieces.append(lax.ppermute(outgoing[shift], "uv", perm))
    return jnp.stack(pieces)


def per_device(visibility, anchor, offset, slot_rows, counts):
    time_groups = lax.axis_size("tm")
    uv_size = lax.axis_size("uv")
    cell_share = TS * TS // time_groups
    vis_rows = visibility[0]
    row_count, row_width = vis_rows.shape
    tile_count, slot_depth = slot_rows.shape[2:]
    slot_size = tile_count * slot_depth
    lanes = max(row_count, slot_depth, tile_count)
    pad = lambda x: jnp.pad(x, ((0, 0), (0, lanes - x.shape[1])))
    (ints,) = lax.optimization_barrier(
        (
            jnp.concatenate(
                [pad(slot_rows[0, 0]), pad(counts[0]), pad(anchor), pad(offset)], axis=0
            ),
        )
    )
    slot_table = ints[:tile_count, :slot_depth]
    live_count = ints[tile_count, :tile_count]
    anchor_row = ints[tile_count + 1, :row_count]
    offset_row = ints[tile_count + 2, :row_count]
    if uv_size <= 16:
        uv_index = lax.axis_index("uv")
        slot_table = lax.dynamic_slice_in_dim(
            jnp.concatenate([slot_table, slot_table], axis=0), uv_index, tile_count, 0
        )
        live_count = lax.dynamic_slice_in_dim(
            jnp.concatenate([live_count, live_count], axis=0), uv_index, tile_count, 0
        )
    is_live = (jnp.arange(slot_depth, dtype=jnp.int32)[None, :] < live_count[:, None]).reshape(-1)
    flat_index = slot_table.reshape(-1)
    pick = (
        (flat_index[:, None] == jnp.arange(row_count, dtype=jnp.int32)[None, :]) & is_live[:, None]
    ).astype(jnp.bfloat16)
    picked = jnp.dot(pick, vis_rows, preferred_element_type=jnp.float32).astype(jnp.bfloat16)
    meta_rows = jnp.concatenate(
        [anchor_row[None, :], offset_row[None, :], jnp.zeros((META - 2, row_count), jnp.int32)],
        axis=0,
    ).astype(jnp.bfloat16)
    meta = lax.dot_general(
        pick, meta_rows, (((1,), (1,)), ((), ())), preferred_element_type=jnp.float32
    ).astype(jnp.bfloat16)
    outgoing = jnp.concatenate([picked, meta], axis=1).reshape(tile_count, slot_depth, row_width + META)
    arrived = uv_exchange(outgoing, uv_size)
    arrived = arrived.reshape(-1, row_width + META)
    arr_anchor = arrived[:, row_width].astype(jnp.int32)
    arr_offset = arrived[:, row_width + 1].astype(jnp.int32)
    tm_index = lax.axis_index("tm")
    pow2 = time_groups & (time_groups - 1) == 0
    if pow2:
        cells = halving_order(tm_index, time_groups, cell_share)
    else:
        cells = jnp.arange(TS * TS, dtype=jnp.int32)
    weights = tap_matrix(cells, arr_anchor, arr_offset)
    partial = jnp.dot(weights, arrived[:, :row_width], preferred_element_type=jnp.float32)
    if pow2:
        summed = halving_reduce(partial, time_groups)
    else:
        summed = lax.psum_scatter(partial, "tm", scatter_dimension=0, tiled=True)
    grid = summed.astype(jnp.bfloat16)
    grid_re, grid_im = grid[:, :NCH], grid[:, NCH:]
    lhs = jnp.concatenate(
        [grid, jnp.concatenate([grid_im, -grid_re], axis=1)], axis=0
    )
    out_scale = 4.0 / math.sqrt(NCH * time_groups * ROWS_DEV)
    both = jnp.dot(lhs, delay_halves(), preferred_element_type=jnp.float32) * out_scale
    cells_out = grid.shape[0]
    return jnp.concatenate([both[:cells_out], both[cells_out:]], axis=1)


def solution(mesh):
    in_specs = (
        P("tm", "uv", None),
        P("tm", "uv"),
        P("tm", "uv"),
        P("tm", "uv", None, None),
        P("tm", "uv", None),
    )
    out_specs = P(("uv", "tm"), None)
    return jax.shard_map(
        per_device, mesh=mesh, in_specs=in_specs, out_specs=out_specs, check_vma=False
    )
```

```python
import math

import jax
import jax.numpy as jnp
from jax import lax
from jax.sharding import PartitionSpec as P

NCH = 1024
ROWS_DEV = 128
TS = 16
KTAPS = 8
OSAMP = 8
META = 128
SPLIT = 32


def kernel_taps(offsets):
    tap_index = jnp.arange(KTAPS, dtype=jnp.float32)
    sub_shift = (offsets.astype(jnp.float32) + 0.5) / OSAMP
    distance = tap_index[None, :] - (KTAPS / 2 - 1.0) - sub_shift[:, None]
    return jnp.exp(-distance * distance / (2.0 * 1.2 * 1.2))


def tap_matrix(cell_ids, anchors, offsets):
    span = TS - KTAPS + 1
    anchor_y = anchors // span
    anchor_x = anchors % span
    taps_y = kernel_taps(offsets // OSAMP)
    taps_x = kernel_taps(offsets % OSAMP)
    cell_y = cell_ids // TS
    cell_x = cell_ids % TS
    along_y = jnp.zeros((cell_ids.shape[0], anchors.shape[0]), jnp.float32)
    along_x = jnp.zeros((cell_ids.shape[0], anchors.shape[0]), jnp.float32)
    for step in range(KTAPS):
        along_y = along_y + jnp.where(
            cell_y[:, None] == anchor_y[None, :] + step, taps_y[None, :, step], 0.0
        )
        along_x = along_x + jnp.where(
            cell_x[:, None] == anchor_x[None, :] + step, taps_x[None, :, step], 0.0
        )
    return (along_y * along_x).astype(jnp.bfloat16)


def delay_halves():
    freq = jnp.arange(NCH, dtype=jnp.int32)
    hi = jnp.arange(NCH // SPLIT, dtype=jnp.int32)
    lo = jnp.arange(SPLIT, dtype=jnp.int32)
    scale = 2.0 * math.pi / NCH
    ang_hi = scale * ((freq[:, None] * (SPLIT * hi)[None, :]) % NCH).astype(jnp.float32)
    ang_lo = scale * ((freq[:, None] * lo[None, :]) % NCH).astype(jnp.float32)
    c_hi, s_hi = jnp.cos(ang_hi), jnp.sin(ang_hi)
    c_lo, s_lo = jnp.cos(ang_lo), jnp.sin(ang_lo)
    cosine = c_hi[:, :, None] * c_lo[:, None, :] - s_hi[:, :, None] * s_lo[:, None, :]
    sine = s_hi[:, :, None] * c_lo[:, None, :] + c_hi[:, :, None] * s_lo[:, None, :]
    window_arg = 2.0 * math.pi * freq.astype(jnp.float32) / (NCH - 1)
    taper = (
        0.35875
        - 0.48829 * jnp.cos(window_arg)
        + 0.14128 * jnp.cos(2.0 * window_arg)
        - 0.01168 * jnp.cos(3.0 * window_arg)
    )
    tap_cos = (taper[:, None, None] * cosine).reshape(NCH, NCH)
    tap_sin = (taper[:, None, None] * sine).reshape(NCH, NCH)
    return jnp.concatenate([tap_cos, tap_sin], axis=0).astype(jnp.bfloat16)


def halving_order(tm_index, time_groups, cell_share):
    level_bits = int(math.log2(time_groups))
    quarter = jnp.zeros((time_groups,), jnp.int32)
    for j in range(time_groups):
        value = tm_index
        pos = j
        for level in range(level_bits):
            half = time_groups >> (level + 1)
            sent = pos < half
            bit = 1 << level
            value = jnp.where(sent, value ^ bit, value)
            pos = pos % half if half > 0 else pos
        quarter = quarter.at[j].set(value)
    cells = quarter[:, None] * cell_share + jnp.arange(cell_share, dtype=jnp.int32)[None, :]
    return cells.reshape(-1)


def halving_reduce(partial, time_groups):
    level_bits = int(math.log2(time_groups))
    if level_bits == 2:
        share = partial.shape[0] // 4
        near = [(i, i ^ 1) for i in range(time_groups)]
        far = [(i, i ^ 2) for i in range(time_groups)]
        first = lax.ppermute(partial[:share], "tm", near)
        second = lax.ppermute(partial[share:2 * share], "tm", near)
        forward = partial[2 * share:3 * share] + first
        received = lax.ppermute(forward.astype(jnp.bfloat16), "tm", far)
        return (partial[3 * share:] + second) + received.astype(jnp.float32)
    for level in range(level_bits):
        half = partial.shape[0] // 2
        bit = 1 << level
        perm = [(i, i ^ bit) for i in range(time_groups)]
        outgoing = partial[:half]
        if level > 0:
            outgoing = outgoing.astype(jnp.bfloat16)
        received = lax.ppermute(outgoing, "tm", perm)
        partial = partial[half:] + received.astype(jnp.float32)
    return partial


def uv_exchange(outgoing, uv_size):
    if uv_size > 16:
        return lax.all_to_all(outgoing, "uv", split_axis=0, concat_axis=0, tiled=True)
    pieces = [outgoing[0]]
    for shift in range(1, uv_size):
        perm = [(i, (i + shift) % uv_size) for i in range(uv_size)]
        pieces.append(lax.ppermute(outgoing[shift], "uv", perm))
    return jnp.stack(pieces)


def per_device(visibility, anchor, offset, slot_rows, counts):
    time_groups = lax.axis_size("tm")
    uv_size = lax.axis_size("uv")
    cell_share = TS * TS // time_groups
    vis_rows = visibility[0]
    row_count, row_width = vis_rows.shape
    tile_count, slot_depth = slot_rows.shape[2:]
    slot_size = tile_count * slot_depth
    lanes = max(row_count, slot_depth, tile_count)
    pad = lambda x: jnp.pad(x, ((0, 0), (0, lanes - x.shape[1])))
    (ints,) = lax.optimization_barrier(
        (
            jnp.concatenate(
                [pad(slot_rows[0, 0]), pad(counts[0]), pad(anchor), pad(offset)], axis=0
            ),
        )
    )
    slot_table = ints[:tile_count, :slot_depth]
    live_count = ints[tile_count, :tile_count]
    anchor_row = ints[tile_count + 1, :row_count]
    offset_row = ints[tile_count + 2, :row_count]
    if uv_size <= 16:
        uv_index = lax.axis_index("uv")
        slot_table = lax.dynamic_slice_in_dim(
            jnp.concatenate([slot_table, slot_table], axis=0), uv_index, tile_count, 0
        )
        live_count = lax.dynamic_slice_in_dim(
            jnp.concatenate([live_count, live_count], axis=0), uv_index, tile_count, 0
        )
    is_live = (jnp.arange(slot_depth, dtype=jnp.int32)[None, :] < live_count[:, None]).reshape(-1)
    flat_index = slot_table.reshape(-1)
    pick = (
        (flat_index[:, None] == jnp.arange(row_count, dtype=jnp.int32)[None, :]) & is_live[:, None]
    ).astype(jnp.bfloat16)
    picked = jnp.dot(pick, vis_rows, preferred_element_type=jnp.float32).astype(jnp.bfloat16)
    meta_rows = jnp.concatenate(
        [anchor_row[None, :], offset_row[None, :], jnp.zeros((META - 2, row_count), jnp.int32)],
        axis=0,
    ).astype(jnp.bfloat16)
    meta = lax.dot_general(
        pick, meta_rows, (((1,), (1,)), ((), ())), preferred_element_type=jnp.float32
    ).astype(jnp.bfloat16)
    outgoing = jnp.concatenate([picked, meta], axis=1).reshape(tile_count, slot_depth, row_width + META)
    arrived = uv_exchange(outgoing, uv_size)
    arrived = arrived.reshape(-1, row_width + META)
    arr_anchor = arrived[:, row_width].astype(jnp.int32)
    arr_offset = arrived[:, row_width + 1].astype(jnp.int32)
    tm_index = lax.axis_index("tm")
    pow2 = time_groups & (time_groups - 1) == 0
    if pow2:
        cells = halving_order(tm_index, time_groups, cell_share)
    else:
        cells = jnp.arange(TS * TS, dtype=jnp.int32)
    weights = tap_matrix(cells, arr_anchor, arr_offset)
    partial = jnp.dot(weights, arrived[:, :row_width], preferred_element_type=jnp.float32)
    if pow2:
        summed = halving_reduce(partial, time_groups)
    else:
        summed = lax.psum_scatter(partial, "tm", scatter_dimension=0, tiled=True)
    grid = summed.astype(jnp.bfloat16)
    grid_re, grid_im = grid[:, :NCH], grid[:, NCH:]
    lhs = jnp.concatenate(
        [grid, jnp.concatenate([grid_im, -grid_re], axis=1)], axis=0
    )
    out_scale = 4.0 / math.sqrt(NCH * time_groups * ROWS_DEV)
    both = jnp.dot(lhs, delay_halves(), preferred_element_type=jnp.float32) * out_scale
    cells_out = grid.shape[0]
    return jnp.concatenate([both[:cells_out], both[cells_out:]], axis=1)


def solution(mesh):
    in_specs = (
        P("tm", "uv", None),
        P("tm", "uv"),
        P("tm", "uv"),
        P("tm", "uv", None, None),
        P("tm", "uv", None),
    )
    out_specs = P(("uv", "tm"), None)
    return jax.shard_map(
        per_device, mesh=mesh, in_specs=in_specs, out_specs=out_specs, check_vma=False
    )
```

```python
import math

import jax
import jax.numpy as jnp
from jax import lax
from jax.sharding import PartitionSpec as P

NCH = 1024
ROWS_DEV = 128
TS = 16
KTAPS = 8
OSAMP = 8
META = 128
SPLIT = 32


def kernel_taps(offsets):
    tap_index = jnp.arange(KTAPS, dtype=jnp.float32)
    sub_shift = (offsets.astype(jnp.float32) + 0.5) / OSAMP
    distance = tap_index[None, :] - (KTAPS / 2 - 1.0) - sub_shift[:, None]
    return jnp.exp(-distance * distance / (2.0 * 1.2 * 1.2))


def tap_matrix(cell_ids, anchors, offsets):
    span = TS - KTAPS + 1
    anchor_y = anchors // span
    anchor_x = anchors % span
    taps_y = kernel_taps(offsets // OSAMP)
    taps_x = kernel_taps(offsets % OSAMP)
    cell_y = cell_ids // TS
    cell_x = cell_ids % TS
    along_y = jnp.zeros((cell_ids.shape[0], anchors.shape[0]), jnp.float32)
    along_x = jnp.zeros((cell_ids.shape[0], anchors.shape[0]), jnp.float32)
    for step in range(KTAPS):
        along_y = along_y + jnp.where(
            cell_y[:, None] == anchor_y[None, :] + step, taps_y[None, :, step], 0.0
        )
        along_x = along_x + jnp.where(
            cell_x[:, None] == anchor_x[None, :] + step, taps_x[None, :, step], 0.0
        )
    return (along_y * along_x).astype(jnp.bfloat16)


def delay_halves():
    freq = jnp.arange(NCH, dtype=jnp.int32)
    hi = jnp.arange(NCH // SPLIT, dtype=jnp.int32)
    lo = jnp.arange(SPLIT, dtype=jnp.int32)
    scale = 2.0 * math.pi / NCH
    ang_hi = scale * ((freq[:, None] * (SPLIT * hi)[None, :]) % NCH).astype(jnp.float32)
    ang_lo = scale * ((freq[:, None] * lo[None, :]) % NCH).astype(jnp.float32)
    c_hi, s_hi = jnp.cos(ang_hi), jnp.sin(ang_hi)
    c_lo, s_lo = jnp.cos(ang_lo), jnp.sin(ang_lo)
    window_arg = 2.0 * math.pi * freq.astype(jnp.float32) / (NCH - 1)
    taper = (
        0.35875
        - 0.48829 * jnp.cos(window_arg)
        + 0.14128 * jnp.cos(2.0 * window_arg)
        - 0.01168 * jnp.cos(3.0 * window_arg)
    )
    wc_hi, ws_hi = taper[:, None] * c_hi, taper[:, None] * s_hi
    tap_cos = (wc_hi[:, :, None] * c_lo[:, None, :] - ws_hi[:, :, None] * s_lo[:, None, :]).reshape(NCH, NCH)
    tap_sin = (ws_hi[:, :, None] * c_lo[:, None, :] + wc_hi[:, :, None] * s_lo[:, None, :]).reshape(NCH, NCH)
    return jnp.concatenate([tap_cos, tap_sin], axis=0).astype(jnp.bfloat16)


def halving_order(tm_index, time_groups, cell_share):
    level_bits = int(math.log2(time_groups))
    quarter = jnp.zeros((time_groups,), jnp.int32)
    for j in range(time_groups):
        value = tm_index
        pos = j
        for level in range(level_bits):
            half = time_groups >> (level + 1)
            sent = pos < half
            bit = 1 << level
            value = jnp.where(sent, value ^ bit, value)
            pos = pos % half if half > 0 else pos
        quarter = quarter.at[j].set(value)
    cells = quarter[:, None] * cell_share + jnp.arange(cell_share, dtype=jnp.int32)[None, :]
    return cells.reshape(-1)


def halving_reduce(partial, time_groups):
    level_bits = int(math.log2(time_groups))
    for level in range(level_bits):
        half = partial.shape[0] // 2
        bit = 1 << level
        perm = [(i, i ^ bit) for i in range(time_groups)]
        outgoing = partial[:half].astype(jnp.bfloat16)
        received = lax.ppermute(outgoing, "tm", perm)
        partial = partial[half:] + received.astype(jnp.float32)
    return partial


def uv_exchange(outgoing, uv_size):
    if uv_size > 16:
        return lax.all_to_all(outgoing, "uv", split_axis=0, concat_axis=0, tiled=True)
    pieces = [outgoing[0]]
    for shift in range(1, uv_size):
        perm = [(i, (i + shift) % uv_size) for i in range(uv_size)]
        pieces.append(lax.ppermute(outgoing[shift], "uv", perm))
    return jnp.stack(pieces)


def per_device(visibility, anchor, offset, slot_rows, counts):
    time_groups = lax.axis_size("tm")
    uv_size = lax.axis_size("uv")
    cell_share = TS * TS // time_groups
    vis_rows = visibility[0]
    row_count, row_width = vis_rows.shape
    tile_count, slot_depth = slot_rows.shape[2:]
    slot_size = tile_count * slot_depth
    lanes = max(row_count, slot_depth, tile_count)
    pad = lambda x: jnp.pad(x, ((0, 0), (0, lanes - x.shape[1])))
    (ints,) = lax.optimization_barrier(
        (
            jnp.concatenate(
                [pad(slot_rows[0, 0]), pad(counts[0]), pad(anchor), pad(offset)], axis=0
            ),
        )
    )
    slot_table = ints[:tile_count, :slot_depth]
    live_count = ints[tile_count, :tile_count]
    anchor_row = ints[tile_count + 1, :row_count]
    offset_row = ints[tile_count + 2, :row_count]
    if uv_size <= 16:
        uv_index = lax.axis_index("uv")
        slot_table = lax.dynamic_slice_in_dim(
            jnp.concatenate([slot_table, slot_table], axis=0), uv_index, tile_count, 0
        )
        live_count = lax.dynamic_slice_in_dim(
            jnp.concatenate([live_count, live_count], axis=0), uv_index, tile_count, 0
        )
    is_live = (jnp.arange(slot_depth, dtype=jnp.int32)[None, :] < live_count[:, None]).reshape(-1)
    flat_index = slot_table.reshape(-1)
    pick = (
        (flat_index[:, None] == jnp.arange(row_count, dtype=jnp.int32)[None, :]) & is_live[:, None]
    ).astype(jnp.bfloat16)
    picked = jnp.dot(pick, vis_rows, preferred_element_type=jnp.float32).astype(jnp.bfloat16)
    meta_rows = jnp.concatenate(
        [anchor_row[None, :], offset_row[None, :], jnp.zeros((META - 2, row_count), jnp.int32)],
        axis=0,
    ).astype(jnp.bfloat16)
    meta = lax.dot_general(
        pick, meta_rows, (((1,), (1,)), ((), ())), preferred_element_type=jnp.float32
    ).astype(jnp.bfloat16)
    outgoing = jnp.concatenate([picked, meta], axis=1).reshape(tile_count, slot_depth, row_width + META)
    arrived = uv_exchange(outgoing, uv_size)
    arrived = arrived.reshape(-1, row_width + META)
    arr_anchor = arrived[:, row_width].astype(jnp.int32)
    arr_offset = arrived[:, row_width + 1].astype(jnp.int32)
    tm_index = lax.axis_index("tm")
    pow2 = time_groups & (time_groups - 1) == 0
    if pow2:
        cells = halving_order(tm_index, time_groups, cell_share)
    else:
        cells = jnp.arange(TS * TS, dtype=jnp.int32)
    weights = tap_matrix(cells, arr_anchor, arr_offset)
    partial = jnp.dot(weights, arrived[:, :row_width], preferred_element_type=jnp.float32)
    if pow2:
        summed = halving_reduce(partial, time_groups)
    else:
        summed = lax.psum_scatter(partial, "tm", scatter_dimension=0, tiled=True)
    grid = summed.astype(jnp.bfloat16)
    grid_re, grid_im = grid[:, :NCH], grid[:, NCH:]
    lhs = jnp.concatenate(
        [grid, jnp.concatenate([grid_im, -grid_re], axis=1)], axis=0
    )
    out_scale = 4.0 / math.sqrt(NCH * time_groups * ROWS_DEV)
    both = jnp.dot(lhs, delay_halves(), preferred_element_type=jnp.float32) * out_scale
    cells_out = grid.shape[0]
    return jnp.concatenate([both[:cells_out], both[cells_out:]], axis=1)


def solution(mesh):
    in_specs = (
        P("tm", "uv", None),
        P("tm", "uv"),
        P("tm", "uv"),
        P("tm", "uv", None, None),
        P("tm", "uv", None),
    )
    out_specs = P(("uv", "tm"), None)
    return jax.shard_map(
        per_device, mesh=mesh, in_specs=in_specs, out_specs=out_specs, check_vma=False
    )
```

```python
import math

import jax
import jax.numpy as jnp
from jax import lax
from jax.sharding import PartitionSpec as P

NCH = 1024
ROWS_DEV = 128
TS = 16
KTAPS = 8
OSAMP = 8
META = 128
SPLIT = 32


def kernel_taps(offsets):
    tap_index = jnp.arange(KTAPS, dtype=jnp.float32)
    sub_shift = (offsets.astype(jnp.float32) + 0.5) / OSAMP
    distance = tap_index[None, :] - (KTAPS / 2 - 1.0) - sub_shift[:, None]
    return jnp.exp(-distance * distance / (2.0 * 1.2 * 1.2))


def tap_matrix(cell_ids, anchors, offsets):
    span = TS - KTAPS + 1
    anchor_y = anchors // span
    anchor_x = anchors % span
    taps_y = kernel_taps(offsets // OSAMP)
    taps_x = kernel_taps(offsets % OSAMP)
    cell_y = cell_ids // TS
    cell_x = cell_ids % TS
    along_y = jnp.zeros((cell_ids.shape[0], anchors.shape[0]), jnp.float32)
    along_x = jnp.zeros((cell_ids.shape[0], anchors.shape[0]), jnp.float32)
    for step in range(KTAPS):
        along_y = along_y + jnp.where(
            cell_y[:, None] == anchor_y[None, :] + step, taps_y[None, :, step], 0.0
        )
        along_x = along_x + jnp.where(
            cell_x[:, None] == anchor_x[None, :] + step, taps_x[None, :, step], 0.0
        )
    return (along_y * along_x).astype(jnp.bfloat16)


def delay_halves():
    freq = jnp.arange(NCH, dtype=jnp.int32)
    hi = jnp.arange(NCH // SPLIT, dtype=jnp.int32)
    lo = jnp.arange(SPLIT, dtype=jnp.int32)
    scale = 2.0 * math.pi / NCH
    ang_hi = scale * ((freq[:, None] * (SPLIT * hi)[None, :]) % NCH).astype(jnp.float32)
    ang_lo = scale * ((freq[:, None] * lo[None, :]) % NCH).astype(jnp.float32)
    c_hi, s_hi = jnp.cos(ang_hi), jnp.sin(ang_hi)
    c_lo, s_lo = jnp.cos(ang_lo), jnp.sin(ang_lo)
    cosine = c_hi[:, :, None] * c_lo[:, None, :] - s_hi[:, :, None] * s_lo[:, None, :]
    sine = s_hi[:, :, None] * c_lo[:, None, :] + c_hi[:, :, None] * s_lo[:, None, :]
    window_arg = 2.0 * math.pi * freq.astype(jnp.float32) / (NCH - 1)
    taper = (
        0.35875
        - 0.48829 * jnp.cos(window_arg)
        + 0.14128 * jnp.cos(2.0 * window_arg)
        - 0.01168 * jnp.cos(3.0 * window_arg)
    )
    tap_cos = (taper[:, None, None] * cosine).reshape(NCH, NCH)
    tap_sin = (taper[:, None, None] * sine).reshape(NCH, NCH)
    return jnp.concatenate([tap_cos, tap_sin], axis=0).astype(jnp.bfloat16)


def halving_order(tm_index, time_groups, cell_share):
    level_bits = int(math.log2(time_groups))
    quarter = jnp.zeros((time_groups,), jnp.int32)
    for j in range(time_groups):
        value = tm_index
        pos = j
        for level in range(level_bits):
            half = time_groups >> (level + 1)
            sent = pos < half
            bit = 1 << level
            value = jnp.where(sent, value ^ bit, value)
            pos = pos % half if half > 0 else pos
        quarter = quarter.at[j].set(value)
    cells = quarter[:, None] * cell_share + jnp.arange(cell_share, dtype=jnp.int32)[None, :]
    return cells.reshape(-1)


def halving_reduce(partial, time_groups):
    level_bits = int(math.log2(time_groups))
    for level in range(level_bits):
        half = partial.shape[0] // 2
        bit = 1 << level
        perm = [(i, i ^ bit) for i in range(time_groups)]
        outgoing = partial[:half].astype(jnp.bfloat16)
        received = lax.ppermute(outgoing, "tm", perm)
        partial = partial[half:] + received.astype(jnp.float32)
    return partial


def uv_exchange(outgoing, uv_size):
    if uv_size > 16:
        return lax.all_to_all(outgoing, "uv", split_axis=0, concat_axis=0, tiled=True)
    pieces = [outgoing[0]]
    for shift in range(1, uv_size):
        perm = [(i, (i + shift) % uv_size) for i in range(uv_size)]
        pieces.append(lax.ppermute(outgoing[shift], "uv", perm))
    return jnp.stack(pieces)


def per_device(visibility, anchor, offset, slot_rows, counts):
    time_groups = lax.axis_size("tm")
    uv_size = lax.axis_size("uv")
    cell_share = TS * TS // time_groups
    vis_rows = visibility[0]
    row_count, row_width = vis_rows.shape
    tile_count, slot_depth = slot_rows.shape[2:]
    slot_size = tile_count * slot_depth
    lanes = max(row_count, slot_depth, tile_count)
    pad = lambda x: jnp.pad(x, ((0, 0), (0, lanes - x.shape[1])))
    (ints,) = lax.optimization_barrier(
        (
            jnp.concatenate(
                [pad(slot_rows[0, 0]), pad(counts[0]), pad(anchor), pad(offset)], axis=0
            ),
        )
    )
    slot_table = ints[:tile_count, :slot_depth]
    live_count = ints[tile_count, :tile_count]
    anchor_row = ints[tile_count + 1, :row_count]
    offset_row = ints[tile_count + 2, :row_count]
    if uv_size <= 16:
        uv_index = lax.axis_index("uv")
        slot_table = lax.dynamic_slice_in_dim(
            jnp.concatenate([slot_table, slot_table], axis=0), uv_index, tile_count, 0
        )
        live_count = lax.dynamic_slice_in_dim(
            jnp.concatenate([live_count, live_count], axis=0), uv_index, tile_count, 0
        )
    is_live = (jnp.arange(slot_depth, dtype=jnp.int32)[None, :] < live_count[:, None]).reshape(-1)
    flat_index = slot_table.reshape(-1)
    pick = (
        (flat_index[:, None] == jnp.arange(row_count, dtype=jnp.int32)[None, :]) & is_live[:, None]
    ).astype(jnp.bfloat16)
    picked = jnp.dot(pick, vis_rows, preferred_element_type=jnp.float32).astype(jnp.bfloat16)
    meta_rows = jnp.concatenate(
        [anchor_row[None, :], offset_row[None, :], jnp.zeros((META - 2, row_count), jnp.int32)],
        axis=0,
    ).astype(jnp.bfloat16)
    meta = lax.dot_general(
        pick, meta_rows, (((1,), (1,)), ((), ())), preferred_element_type=jnp.float32
    ).astype(jnp.bfloat16)
    outgoing = jnp.concatenate([picked, meta], axis=1).reshape(tile_count, slot_depth, row_width + META)
    arrived = uv_exchange(outgoing, uv_size)
    arrived = arrived.reshape(-1, row_width + META)
    arr_anchor = arrived[:, row_width].astype(jnp.int32)
    arr_offset = arrived[:, row_width + 1].astype(jnp.int32)
    tm_index = lax.axis_index("tm")
    pow2 = time_groups & (time_groups - 1) == 0
    if pow2:
        cells = halving_order(tm_index, time_groups, cell_share)
    else:
        cells = jnp.arange(TS * TS, dtype=jnp.int32)
    weights = tap_matrix(cells, arr_anchor, arr_offset)
    partial = jnp.dot(weights, arrived[:, :row_width], preferred_element_type=jnp.float32)
    if pow2:
        summed = halving_reduce(partial, time_groups)
    else:
        summed = lax.psum_scatter(partial, "tm", scatter_dimension=0, tiled=True)
    grid = summed.astype(jnp.bfloat16)
    grid_re, grid_im = grid[:, :NCH], grid[:, NCH:]
    lhs = jnp.concatenate(
        [grid, jnp.concatenate([grid_im, -grid_re], axis=1)], axis=0
    )
    out_scale = 4.0 / math.sqrt(NCH * time_groups * ROWS_DEV)
    both = jnp.dot(lhs, delay_halves(), preferred_element_type=jnp.float32) * out_scale
    cells_out = grid.shape[0]
    return jnp.concatenate([both[:cells_out], both[cells_out:]], axis=1)


def solution(mesh):
    in_specs = (
        P("tm", "uv", None),
        P("tm", "uv"),
        P("tm", "uv"),
        P("tm", "uv", None, None),
        P("tm", "uv", None),
    )
    out_specs = P(("uv", "tm"), None)
    return jax.shard_map(
        per_device, mesh=mesh, in_specs=in_specs, out_specs=out_specs, check_vma=False
    )
```
